256 devices in a mesh: member: 8 (over x, y_hi), space: 32 (over y_lo, z, core).
Axes of the slice: x: 4, y: 4 (y_hi: 2, y_lo: 2; y = y_hi * 2 + y_lo), z: 8, core: 2. Of those that a mesh axis runs over, the one named last changes fastest.
Arguments:
- ensemble: bfloat16 [256, 48, 16384], P('member', None, 'space')
- inflation: float32 [256, 128], P('member'), may hold values from 0.5 to 2
- weights: bfloat16 [128, 256, 256], P('space')
- region_ids: int32 [16384], P('space'), may hold values from 0 to 127, as said below
- extinction: float32 [48], replicated, may hold values from 0.1 to 2
- obs_cols: int32 [4096], P('space'), may hold values from 0 to 16383, as said below
Outputs:
- analysis: bfloat16 [256, 48, 16384], P('member', None, 'space')
- obs_analysis: float32 [256, 4096], P('member', 'space')
The draws below stay inside these ranges and needn't reach their ends.
Inputs may be any that keep to these rules, and one draw needn't show every extreme that they name: `region_ids`: region r belongs to index r // 4 of space. Each block of 512 columns held by one index of space holds exactly 16 columns of the regions of every index of space. `obs_cols`: each observation's column lies in the block of 512 columns held by the same index of space as the observation.
All inputs are finite; a program needn't handle non-finite values.
Results may differ from the reference program's by a relative error of at most 0.0047.
Values may be sent and summed in bfloat16 or wider, within the bound.
No kernel may reach another device: no remote copies, remote signals or barrier semaphores. Data moves between devices by JAX's collectives and lax.ppermute only.
A program may use at most 64 MiB of HBM per device.

```python
import math
import jax
import jax.numpy as jnp
from jax import lax

K = 256
TR = 48
C_DEV = 512
REG_DEV = 4
OBS_DEV = 128
NCOL = 16384
REGIONS = 128
NOBS = 4096
N_SPACE = 32


def draw_ensemble(key, part):
    first, second = jax.random.split(jax.random.fold_in(key, 11))
    center = 2.0 * jax.random.normal(first, (TR, NCOL), jnp.float32)
    spread = jax.random.normal(second, (K, TR, NCOL), jnp.float32)
    return (center[None] + spread).astype(jnp.bfloat16)


def draw_weights(key, part):
    first, second = jax.random.split(jax.random.fold_in(key, 23))
    diag = jax.random.uniform(first, (REGIONS, K), jnp.float32, 0.6, 1.4)
    noise = jax.random.normal(second, (REGIONS, K, K), jnp.float32) * (0.9 / K ** 0.5)
    eye = jnp.eye(K, dtype=jnp.float32)
    return (noise + diag[:, :, None] * eye[None]).astype(jnp.bfloat16)


def draw_region_ids(key, part):
    keys = jax.random.split(jax.random.fold_in(key, 37), N_SPACE)

    def one_shard(shard_key):
        first, second = jax.random.split(shard_key)
        owners = jnp.arange(C_DEV, dtype=jnp.int32) % N_SPACE
        owners = owners[jax.random.permutation(first, C_DEV)]
        local = jax.random.randint(second, (C_DEV,), 0, REG_DEV, dtype=jnp.int32)
        return owners * REG_DEV + local
    return jax.vmap(one_shard)(keys).reshape(NCOL)


def draw_obs_cols(key, part):
    offsets = jax.random.randint(jax.random.fold_in(key, 41), (N_SPACE, OBS_DEV), 0, C_DEV, dtype=jnp.int32)
    offsets = offsets.at[0, 0].set(0)
    offsets = offsets.at[N_SPACE - 1, OBS_DEV - 1].set(C_DEV - 1)
    bases = jnp.arange(N_SPACE, dtype=jnp.int32)[:, None] * C_DEV
    return (bases + offsets).reshape(NOBS)


def block_levels(stream_key, extent, shards, smallest, high):
    loudness, own = 1.0, jax.random.fold_in(stream_key, 6)
    for axis_at, shards_of in shards:
        steps = jnp.exp(jax.random.uniform(jax.random.fold_in(own, axis_at), (shards_of,), jnp.float32, smallest / len(shards), high / len(shards)))
        loudness = loudness * jnp.repeat(steps, extent[axis_at] // shards_of).reshape([-1 if axis == axis_at else 1 for axis in range(len(extent))])
    return loudness


def setup_inputs(seed: int = 0) -> dict:
    arg_keys = jax.random.split(jax.random.key(seed), 7)
    return {
        "ensemble": draw_ensemble(jax.random.fold_in(arg_keys[6], 71), 0),
        "inflation": jnp.clip(jnp.exp(math.log(2.0) - 1.3862944 * jax.random.uniform(arg_keys[1], (K, REGIONS), jnp.float32) ** block_levels(arg_keys[1], (K, REGIONS), ((0, 8),), -0.2, 0.2)), 0.5, 2.0),
        "weights": draw_weights(jax.random.fold_in(arg_keys[6], 71), 0),
        "region_ids": draw_region_ids(jax.random.fold_in(arg_keys[6], 71), 0),
        "extinction": jnp.clip(jnp.exp(jax.random.uniform(arg_keys[4], (TR,), jnp.float32, math.log(0.1), math.log(2.0))), 0.1, 2.0),
        "obs_cols": draw_obs_cols(jax.random.fold_in(arg_keys[6], 71), 0),
    }


def reference(ensemble, inflation, weights, region_ids, extinction, obs_cols):
    mean = jnp.sum(ensemble.astype(jnp.float32), axis=0) / K
    nblocks = NCOL // 128

    def one_block(index):
        start = (index * 128).astype(jnp.int32)
        members = lax.dynamic_slice_in_dim(ensemble, start, 128, 2).astype(jnp.float32)
        labels = lax.dynamic_slice_in_dim(region_ids, start, 128, 0)
        center = lax.dynamic_slice_in_dim(mean, start, 128, 1)
        factor = inflation[:, labels]
        anomaly = ((members - center[None]) * factor[:, None, :]).astype(jnp.bfloat16)
        chosen = weights[labels].astype(jnp.float32)
        product = jnp.einsum("cjk,jtc->ktc", chosen, anomaly.astype(jnp.float32), precision=lax.Precision.HIGHEST)
        rounded = lax.optimization_barrier(product.astype(jnp.bfloat16))
        return (center[None] + rounded.astype(jnp.float32)).astype(jnp.bfloat16)

    blocks = lax.map(one_block, jnp.arange(nblocks, dtype=jnp.int32))
    analysis = jnp.transpose(blocks, (1, 2, 0, 3)).reshape(K, TR, NCOL)
    picked = analysis[:, :, obs_cols].astype(jnp.float32)
    obs_analysis = jnp.einsum("t,kto->ko", extinction, picked, precision=lax.Precision.HIGHEST)
    return analysis, obs_analysis
```

```python
import jax
import jax.numpy as jnp
from jax import lax
from jax.sharding import PartitionSpec as P


def _split3(x):
    hi = lax.reduce_precision(x, exponent_bits=8, mantissa_bits=7)
    r1 = x - hi
    mid = lax.reduce_precision(r1, exponent_bits=8, mantissa_bits=7)
    lo = r1 - mid
    return hi.astype(jnp.bfloat16), mid.astype(jnp.bfloat16), lo.astype(jnp.bfloat16)


def local(ensemble, inflation, weights, region_ids, extinction, obs_cols):
    n_space = lax.axis_size("space")
    n_member = lax.axis_size("member")
    local_members = ensemble.shape[0]
    tracers = ensemble.shape[1]
    columns = ensemble.shape[2]
    members = local_members * n_member
    reg_count = weights.shape[0]
    all_regions = inflation.shape[1]
    send_cols = columns // n_space
    slot_cols = send_cols // n_member
    own_cols = n_space * slot_cols
    row_len = local_members * tracers
    extra_len = 128
    owner = region_ids // reg_count
    owner_hot = (owner[:, None] == jnp.arange(n_space, dtype=jnp.int32)[None, :]).astype(jnp.int32)
    before = jnp.cumsum(owner_hot, axis=0) - owner_hot
    rank_in = jnp.sum(before * owner_hot, axis=1)
    position = owner * send_cols + rank_in
    ordering = (
        jnp.zeros((columns,), jnp.int32).at[position].set(jnp.arange(columns, dtype=jnp.int32))
    )
    region_hot = (jnp.arange(all_regions, dtype=jnp.int32)[:, None] == region_ids[None, :]).astype(
        jnp.float32
    )
    factor = jnp.dot(inflation, region_hot, precision=lax.Precision.HIGHEST)
    f_hi, f_mid, f_lo = _split3(factor.T)
    label = (region_ids % reg_count).astype(jnp.bfloat16)[:, None]
    pad = jnp.zeros((columns, extra_len - 3 * local_members - 1), jnp.bfloat16)
    extra = jnp.concatenate([f_hi, f_mid, f_lo, label, pad], axis=1)
    rows_major = jnp.transpose(ensemble, (2, 0, 1)).reshape(columns, row_len)
    rows = jnp.concatenate([rows_major, extra], axis=1)
    width = row_len + extra_len
    payload = jnp.take(rows, ordering, axis=0).reshape(n_space, n_member, slot_cols, width)
    received = lax.all_to_all(
        lax.all_to_all(payload, "member", split_axis=1, concat_axis=3, tiled=True),
        "space",
        split_axis=0,
        concat_axis=0,
        tiled=True,
    )
    gathered = received.reshape(own_cols, n_member, width)
    ens_part = gathered[:, :, :row_len].reshape(own_cols, members, tracers)
    ext = gathered[:, :, row_len:].astype(jnp.float32)
    lm = local_members
    fac = ((ext[:, :, 0:lm] + ext[:, :, lm:2 * lm]) + ext[:, :, 2 * lm:3 * lm]).reshape(
        own_cols, members
    )
    got_labels = ext[:, 0, 3 * lm].astype(jnp.int32)
    ens32 = ens_part.astype(jnp.float32)
    mean = jnp.sum(ens32, axis=1) / members
    anomaly = ((ens32 - mean[:, None, :]) * fac[:, :, None]).astype(jnp.bfloat16)
    accum = jnp.zeros((own_cols, members, tracers), jnp.float32)
    for region in range(reg_count):
        partial_prod = jnp.einsum(
            "jk,cjt->ckt", weights[region], anomaly, preferred_element_type=jnp.float32
        )
        accum = accum + jnp.where((got_labels == region)[:, None, None], partial_prod, 0.0)
    increment = accum.astype(jnp.bfloat16)
    result_rows = (mean[:, None, :] + increment.astype(jnp.float32)).astype(jnp.bfloat16)
    result_rows = result_rows.reshape(n_space, 1, slot_cols, members * tracers)
    halfway = lax.all_to_all(result_rows, "space", split_axis=0, concat_axis=0, tiled=True)
    returned = lax.all_to_all(halfway, "member", split_axis=3, concat_axis=1, tiled=True)
    restored = jnp.take(returned.reshape(columns, local_members * tracers), position, axis=0)
    analysis = jnp.transpose(restored.reshape(columns, local_members, tracers), (1, 2, 0))
    local_index = obs_cols - lax.axis_index("space") * columns
    picked = jnp.take(analysis, local_index, axis=2).astype(jnp.float32)
    obs_analysis = jnp.einsum("t,kto->ko", extinction, picked, precision=lax.Precision.HIGHEST)
    return (analysis, obs_analysis)


def solution(mesh):
    in_specs = (
        P("member", None, "space"),
        P("member", None),
        P("space", None, None),
        P("space"),
        P(),
        P("space"),
    )
    out_specs = (P("member", None, "space"), P("member", "space"))
    return jax.shard_map(local, mesh=mesh, in_specs=in_specs, out_specs=out_specs, check_vma=False)
```

```python
import jax
import jax.numpy as jnp
from jax import lax
from jax.sharding import PartitionSpec as P


def _split3(x):
    hi = lax.reduce_precision(x, exponent_bits=8, mantissa_bits=7)
    r1 = x - hi
    mid = lax.reduce_precision(r1, exponent_bits=8, mantissa_bits=7)
    lo = r1 - mid
    return hi.astype(jnp.bfloat16), mid.astype(jnp.bfloat16), lo.astype(jnp.bfloat16)


def local(ensemble, inflation, weights, region_ids, extinction, obs_cols):
    n_space = lax.axis_size("space")
    n_member = lax.axis_size("member")
    local_members = ensemble.shape[0]
    tracers = ensemble.shape[1]
    columns = ensemble.shape[2]
    members = local_members * n_member
    reg_count = weights.shape[0]
    all_regions = inflation.shape[1]
    groups_per_dev = n_space // n_member
    send_cols = columns // n_space
    own_cols = columns // n_member
    row_len = local_members * tracers
    extra_len = 128
    me_space = lax.axis_index("space")
    me_member = lax.axis_index("member")

    fetched = []
    for q in range(groups_per_dev):
        perm = []
        for m in range(n_member):
            for s in range(n_space):
                src = (s + groups_per_dev * m + q) % n_space
                perm.append((m * n_space + src, m * n_space + s))
        fetched.append(lax.ppermute(weights, ("member", "space"), perm))
    w_all = jnp.stack(fetched)

    owner = region_ids // reg_count
    shift = (owner - me_space) % n_space
    owner_hot = (owner[:, None] == jnp.arange(n_space, dtype=jnp.int32)[None, :]).astype(jnp.int32)
    before = jnp.cumsum(owner_hot, axis=0) - owner_hot
    rank_in = jnp.sum(before * owner_hot, axis=1)
    position = shift * send_cols + rank_in
    ordering = (
        jnp.zeros((columns,), jnp.int32).at[position].set(jnp.arange(columns, dtype=jnp.int32))
    )
    labels_sorted = jnp.take(region_ids % reg_count, ordering).reshape(n_member, own_cols)
    my_labels = lax.dynamic_index_in_dim(labels_sorted, me_member, 0, keepdims=False)

    region_hot = (jnp.arange(all_regions, dtype=jnp.int32)[:, None] == region_ids[None, :]).astype(
        jnp.float32
    )
    factor = jnp.dot(inflation, region_hot, precision=lax.Precision.HIGHEST)
    f_hi, f_mid, f_lo = _split3(factor.T)
    pad = jnp.zeros((columns, extra_len - 3 * local_members), jnp.bfloat16)
    extra = jnp.concatenate([f_hi, f_mid, f_lo, pad], axis=1)
    rows_major = jnp.transpose(ensemble, (2, 0, 1)).reshape(columns, row_len)
    rows = jnp.concatenate([rows_major, extra], axis=1)
    width = row_len + extra_len
    payload = jnp.take(rows, ordering, axis=0).reshape(n_member, own_cols, width)
    received = lax.all_to_all(payload, "member", split_axis=0, concat_axis=0, tiled=True)
    gathered = jnp.transpose(received, (1, 0, 2))
    ens_part = gathered[:, :, :row_len].reshape(own_cols, members, tracers)
    ext = gathered[:, :, row_len:].astype(jnp.float32)
    lm = local_members
    fac = ((ext[:, :, 0:lm] + ext[:, :, lm:2 * lm]) + ext[:, :, 2 * lm:3 * lm]).reshape(
        own_cols, members
    )
    ens32 = ens_part.astype(jnp.float32)
    mean = jnp.sum(ens32, axis=1) / members
    anomaly = ((ens32 - mean[:, None, :]) * fac[:, :, None]).astype(jnp.bfloat16)
    anomaly = anomaly.reshape(groups_per_dev, send_cols, members, tracers)
    labels_g = my_labels.reshape(groups_per_dev, send_cols)
    accum = jnp.zeros((groups_per_dev, send_cols, members, tracers), jnp.float32)
    for region in range(reg_count):
        partial_prod = jnp.einsum(
            "qjk,qcjt->qckt", w_all[:, region], anomaly, preferred_element_type=jnp.float32
        )
        accum = accum + jnp.where((labels_g == region)[:, :, None, None], partial_prod, 0.0)
    increment = lax.reduce_precision(accum, exponent_bits=8, mantissa_bits=7)
    increment = increment.reshape(own_cols, members, tracers)
    result = (mean[:, None, :] + increment).astype(jnp.bfloat16)
    result = jnp.transpose(result.reshape(own_cols, n_member, row_len), (1, 0, 2))
    returned = lax.all_to_all(result, "member", split_axis=0, concat_axis=0, tiled=True)
    restored = jnp.take(returned.reshape(columns, row_len), position, axis=0)
    analysis = jnp.transpose(restored.reshape(columns, local_members, tracers), (1, 2, 0))
    local_index = obs_cols - me_space * columns
    picked = jnp.take(analysis, local_index, axis=2).astype(jnp.float32)
    obs_analysis = jnp.einsum("t,kto->ko", extinction, picked, precision=lax.Precision.HIGHEST)
    return (analysis, obs_analysis)


def solution(mesh):
    in_specs = (
        P("member", None, "space"),
        P("member", None),
        P("space", None, None),
        P("space"),
        P(),
        P("space"),
    )
    out_specs = (P("member", None, "space"), P("member", "space"))
    return jax.shard_map(local, mesh=mesh, in_specs=in_specs, out_specs=out_specs, check_vma=False)
```

```python
import jax
import jax.numpy as jnp
from jax import lax
from jax.sharding import PartitionSpec as P


def local(ensemble, inflation, weights, region_ids, extinction, obs_cols):
    n_space = lax.axis_size("space")
    n_member = lax.axis_size("member")
    local_members, tracers, columns = ensemble.shape
    members = local_members * n_member
    reg_count = weights.shape[0]
    all_regions = inflation.shape[1]
    groups_per_dev = n_space // n_member
    send_cols = columns // n_space
    own_cols = columns // n_member
    n_chip = n_space // 2
    chips_per_dev = groups_per_dev // 2
    n_slot = groups_per_dev * reg_count
    me_space = lax.axis_index("space")
    me_member = lax.axis_index("member")
    chip = me_space // 2
    core = me_space % 2

    own = []
    for a in range(chips_per_dev):
        perm = []
        for m in range(n_member):
            for s in range(n_space):
                src = 2 * ((s // 2 + chips_per_dev * m + a) % n_chip) + s % 2
                perm.append((m * n_space + src, m * n_space + s))
        own.append(lax.ppermute(weights, ("member", "space"), perm))
    own = jnp.stack(own)
    sib_perm = [(m * n_space + s, m * n_space + (s ^ 1)) for m in range(n_member) for s in range(n_space)]
    sib = lax.ppermute(own, ("member", "space"), sib_perm)
    w_all = jnp.concatenate([own, sib], axis=0).reshape(n_slot, members, members)

    group = region_ids // reg_count
    offset = (group // 2 - chip) % n_chip
    dest = offset // chips_per_dev
    slot = (group % 2 != core).astype(jnp.int32) * chips_per_dev + offset % chips_per_dev
    group_hot = (group[:, None] == jnp.arange(n_space, dtype=jnp.int32)[None, :]).astype(jnp.int32)
    before = jnp.cumsum(group_hot, axis=0) - group_hot
    rank_in = jnp.sum(before * group_hot, axis=1)
    position = dest * own_cols + slot * send_cols + rank_in
    label = slot * reg_count + region_ids % reg_count
    pos_iota = jnp.arange(columns, dtype=jnp.int32)
    perm_hot = position[:, None] == pos_iota[None, :]
    perm_mat = perm_hot.astype(jnp.bfloat16).reshape(columns, n_member, own_cols)
    label_sorted = jnp.sum(jnp.where(perm_hot, label[:, None], 0), axis=0).reshape(n_member, own_cols)
    my_labels = lax.dynamic_index_in_dim(label_sorted, me_member, 0, keepdims=False)

    region_hot = (jnp.arange(all_regions, dtype=jnp.int32)[:, None] == region_ids[None, :]).astype(
        jnp.float32
    )
    factor = jnp.dot(inflation, region_hot, precision=lax.Precision.HIGHEST)
    fac_perm = jnp.einsum(
        "jc,cdi->dji", factor, perm_mat.astype(jnp.float32), precision=lax.Precision.HIGHEST
    )
    payload = jnp.einsum("jtc,cdi->djti", ensemble, perm_mat, preferred_element_type=jnp.bfloat16)

    received = lax.all_to_all(payload, "member", split_axis=0, concat_axis=0, tiled=True)
    fac_got = lax.all_to_all(fac_perm, "member", split_axis=0, concat_axis=0, tiled=True)
    ens32 = received.reshape(members, tracers, own_cols).astype(jnp.float32)
    fac = fac_got.reshape(members, own_cols)
    mean = jnp.sum(ens32, axis=0) / members
    anomaly = ((ens32 - mean[None]) * fac[:, None, :]).astype(jnp.bfloat16)
    mask = my_labels[None, :] == jnp.arange(n_slot, dtype=jnp.int32)[:, None]
    masked = jnp.where(mask[:, None, None, :], anomaly[None], jnp.zeros((), jnp.bfloat16))
    inc = jnp.einsum("rjk,rjtc->ktc", w_all, masked, preferred_element_type=jnp.float32)
    inc = lax.reduce_precision(inc, exponent_bits=8, mantissa_bits=7)
    result = (mean[None] + inc).astype(jnp.bfloat16)
    result = result.reshape(n_member, local_members, tracers, own_cols)
    returned = lax.all_to_all(result, "member", split_axis=0, concat_axis=0, tiled=True)
    analysis = jnp.einsum("dkti,cdi->ktc", returned, perm_mat, preferred_element_type=jnp.bfloat16)

    local_index = obs_cols - me_space * columns
    obs_pos = jnp.take(position, local_index)
    obs_mat = (pos_iota[:, None] == obs_pos[None, :]).astype(jnp.bfloat16)
    obs_mat = obs_mat.reshape(n_member, own_cols, obs_cols.shape[0])
    picked = jnp.einsum("dkti,dio->kto", returned, obs_mat, preferred_element_type=jnp.float32)
    obs_analysis = jnp.einsum("t,kto->ko", extinction, picked, precision=lax.Precision.HIGHEST)
    return (analysis, obs_analysis)


def solution(mesh):
    in_specs = (
        P("member", None, "space"),
        P("member", None),
        P("space", None, None),
        P("space"),
        P(),
        P("space"),
    )
    out_specs = (P("member", None, "space"), P("member", "space"))
    return jax.shard_map(local, mesh=mesh, in_specs=in_specs, out_specs=out_specs, check_vma=False)
```

```python
import jax
import jax.numpy as jnp
from jax import lax
from jax.sharding import PartitionSpec as P


def _split3(x):
    hi = lax.reduce_precision(x, exponent_bits=8, mantissa_bits=7)
    r1 = x - hi
    mid = lax.reduce_precision(r1, exponent_bits=8, mantissa_bits=7)
    lo = r1 - mid
    return hi.astype(jnp.bfloat16), mid.astype(jnp.bfloat16), lo.astype(jnp.bfloat16)


def local(ensemble, inflation, weights, region_ids, extinction, obs_cols):
    n_space = lax.axis_size("space")
    n_member = lax.axis_size("member")
    local_members, tracers, columns = ensemble.shape
    members = local_members * n_member
    reg_count = weights.shape[0]
    all_regions = inflation.shape[1]
    groups_per_dev = n_space // n_member
    send_cols = columns // n_space
    own_cols = columns // n_member
    n_chip = n_space // 2
    chips_per_dev = groups_per_dev // 2
    n_slot = groups_per_dev * reg_count
    me_space = lax.axis_index("space")
    me_member = lax.axis_index("member")
    chip = me_space // 2
    core = me_space % 2

    ring = n_chip // 2
    pairs = [(0, ring // 2)] + [(b, ring - b) for b in range(1, ring // 2)]
    pairs = pairs + [(a + ring, b + ring) for a, b in pairs]
    owner_of = [0] * n_chip
    slot_of = [0] * n_chip
    for m, pair in enumerate(pairs):
        for a, off in enumerate(pair):
            owner_of[off] = m
            slot_of[off] = a
    own = []
    for a in range(chips_per_dev):
        perm = []
        for m in range(n_member):
            for s in range(n_space):
                src = 2 * ((s // 2 + pairs[m][a]) % n_chip) + s % 2
                perm.append((m * n_space + src, m * n_space + s))
        own.append(lax.ppermute(weights, ("member", "space"), perm))
    own = jnp.stack(own)
    sib_perm = [(m * n_space + s, m * n_space + (s ^ 1)) for m in range(n_member) for s in range(n_space)]
    sib = lax.ppermute(own, ("member", "space"), sib_perm)
    w_all = jnp.concatenate([own, sib], axis=0).reshape(n_slot, members, members)

    group = region_ids // reg_count
    offset = (group // 2 - chip) % n_chip
    dest = jnp.array(owner_of, jnp.int32)[offset]
    slot = (group % 2 != core).astype(jnp.int32) * chips_per_dev + jnp.array(slot_of, jnp.int32)[offset]
    group_hot = (group[:, None] == jnp.arange(n_space, dtype=jnp.int32)[None, :]).astype(jnp.int32)
    before = jnp.cumsum(group_hot, axis=0) - group_hot
    rank_in = jnp.sum(before * group_hot, axis=1)
    position = dest * own_cols + slot * send_cols + rank_in
    label = slot * reg_count + region_ids % reg_count
    pos_iota = jnp.arange(columns, dtype=jnp.int32)
    perm_hot = position[:, None] == pos_iota[None, :]
    perm_mat = perm_hot.astype(jnp.bfloat16).reshape(columns, n_member, own_cols)
    label_sorted = jnp.sum(jnp.where(perm_hot, label[:, None], 0), axis=0).reshape(n_member, own_cols)
    my_labels = lax.dynamic_index_in_dim(label_sorted, me_member, 0, keepdims=False)

    region_hot = (jnp.arange(all_regions, dtype=jnp.int32)[:, None] == region_ids[None, :]).astype(
        jnp.float32
    )
    factor = jnp.dot(inflation, region_hot, precision=lax.Precision.HIGHEST)
    fac_perm = jnp.einsum(
        "jc,cdi->dji", factor, perm_mat.astype(jnp.float32), precision=lax.Precision.HIGHEST
    )
    main = jnp.einsum("jtc,cdi->djti", ensemble, perm_mat, preferred_element_type=jnp.bfloat16)
    pieces = jnp.stack(_split3(fac_perm), axis=1)
    extra_rows = 3 * local_members // tracers
    pieces = pieces.reshape(n_member, extra_rows, tracers, own_cols)
    payload = jnp.concatenate([main, pieces], axis=1)

    received = lax.all_to_all(payload, "member", split_axis=0, concat_axis=0, tiled=True)
    ens32 = received[:, :local_members].reshape(members, tracers, own_cols).astype(jnp.float32)
    got = received[:, local_members:].reshape(n_member, 3, local_members, own_cols)
    got = got.astype(jnp.float32)
    fac = ((got[:, 0] + got[:, 1]) + got[:, 2]).reshape(members, own_cols)
    mean = jnp.sum(ens32, axis=0) / members
    anomaly = ((ens32 - mean[None]) * fac[:, None, :]).astype(jnp.bfloat16)
    mask = my_labels[None, :] == jnp.arange(n_slot, dtype=jnp.int32)[:, None]
    masked = jnp.where(mask[:, None, None, :], anomaly[None], jnp.zeros((), jnp.bfloat16))
    inc = jnp.einsum("rjk,rjtc->ktc", w_all, masked, preferred_element_type=jnp.float32)
    inc = lax.reduce_precision(inc, exponent_bits=8, mantissa_bits=7)
    result = (mean[None] + inc).astype(jnp.bfloat16)
    result = result.reshape(n_member, local_members, tracers, own_cols)
    returned = lax.all_to_all(result, "member", split_axis=0, concat_axis=0, tiled=True)
    analysis = jnp.einsum("dkti,cdi->ktc", returned, perm_mat, preferred_element_type=jnp.bfloat16)

    local_index = obs_cols - me_space * columns
    obs_pos = jnp.take(position, local_index)
    obs_mat = (pos_iota[:, None] == obs_pos[None, :]).astype(jnp.bfloat16)
    obs_mat = obs_mat.reshape(n_member, own_cols, obs_cols.shape[0])
    picked = jnp.einsum("dkti,dio->kto", returned, obs_mat, preferred_element_type=jnp.float32)
    obs_analysis = jnp.einsum("t,kto->ko", extinction, picked, precision=lax.Precision.HIGHEST)
    return (analysis, obs_analysis)


def solution(mesh):
    in_specs = (
        P("member", None, "space"),
        P("member", None),
        P("space", None, None),
        P("space"),
        P(),
        P("space"),
    )
    out_specs = (P("member", None, "space"), P("member", "space"))
    return jax.shard_map(local, mesh=mesh, in_specs=in_specs, out_specs=out_specs, check_vma=False)
```

```python
import jax
import jax.numpy as jnp
from jax import lax
from jax.sharding import PartitionSpec as P


def _split3(x):
    hi = lax.reduce_precision(x, exponent_bits=8, mantissa_bits=7)
    r1 = x - hi
    mid = lax.reduce_precision(r1, exponent_bits=8, mantissa_bits=7)
    lo = r1 - mid
    return hi.astype(jnp.bfloat16), mid.astype(jnp.bfloat16), lo.astype(jnp.bfloat16)


def local(ensemble, inflation, weights, region_ids, extinction, obs_cols):
    n_space = lax.axis_size("space")
    n_member = lax.axis_size("member")
    local_members, tracers, columns = ensemble.shape
    members = local_members * n_member
    reg_count = weights.shape[0]
    all_regions = inflation.shape[1]
    groups_per_dev = n_space // n_member
    send_cols = columns // n_space
    own_cols = columns // n_member
    n_chip = n_space // 2
    chips_per_dev = groups_per_dev // 2
    n_slot = groups_per_dev * reg_count
    me_space = lax.axis_index("space")
    me_member = lax.axis_index("member")
    chip = me_space // 2
    core = me_space % 2

    ring = n_chip // 2
    pairs = [(0, ring // 2)] + [(b, ring - b) for b in range(1, ring // 2)]
    pairs = pairs + [(a + ring, b + ring) for a, b in pairs]
    owner_of = [0] * n_chip
    slot_of = [0] * n_chip
    for m, pair in enumerate(pairs):
        for a, off in enumerate(pair):
            owner_of[off] = m
            slot_of[off] = a
    own = []
    for a in range(chips_per_dev):
        perm = []
        for m in range(n_member):
            for s in range(n_space):
                src = 2 * ((s // 2 + pairs[m][a]) % n_chip) + s % 2
                perm.append((m * n_space + src, m * n_space + s))
        own.append(lax.ppermute(weights, ("member", "space"), perm))
    own = jnp.stack(own)
    sib_perm = [(m * n_space + s, m * n_space + (s ^ 1)) for m in range(n_member) for s in range(n_space)]
    sib = lax.ppermute(own, ("member", "space"), sib_perm)
    w_all = jnp.concatenate([own, sib], axis=0).reshape(n_slot, members, members)

    group = region_ids // reg_count
    offset = (group // 2 - chip) % n_chip
    dest = jnp.array(owner_of, jnp.int32)[offset]
    slot = (group % 2 != core).astype(jnp.int32) * chips_per_dev + jnp.array(slot_of, jnp.int32)[offset]
    group_hot = (group[:, None] == jnp.arange(n_space, dtype=jnp.int32)[None, :]).astype(jnp.int32)
    before = jnp.cumsum(group_hot, axis=0) - group_hot
    rank_in = jnp.sum(before * group_hot, axis=1)
    position = dest * own_cols + slot * send_cols + rank_in
    label = slot * reg_count + region_ids % reg_count
    pos_iota = jnp.arange(columns, dtype=jnp.int32)
    perm_hot = position[:, None] == pos_iota[None, :]
    perm_mat = perm_hot.astype(jnp.bfloat16).reshape(columns, n_member, own_cols)
    label_sorted = jnp.sum(jnp.where(perm_hot, label[:, None], 0), axis=0).reshape(n_member, own_cols)
    my_labels = lax.dynamic_index_in_dim(label_sorted, me_member, 0, keepdims=False)

    region_hot = (jnp.arange(all_regions, dtype=jnp.int32)[:, None] == region_ids[None, :]).astype(
        jnp.float32
    )
    factor = jnp.dot(inflation, region_hot, precision=lax.Precision.HIGHEST)
    fac_perm = jnp.einsum(
        "jc,cdi->dji", factor, perm_mat.astype(jnp.float32), precision=lax.Precision.HIGHEST
    )
    main = jnp.einsum("jtc,cdi->djti", ensemble, perm_mat, preferred_element_type=jnp.bfloat16)
    pieces = jnp.stack(_split3(fac_perm), axis=1)
    extra_rows = 3 * local_members // tracers
    pieces = pieces.reshape(n_member, extra_rows, tracers, own_cols)
    payload = jnp.concatenate([main, pieces], axis=1)

    received = lax.all_to_all(payload, "member", split_axis=0, concat_axis=0, tiled=True)
    ens = received[:, :local_members].reshape(members, tracers, own_cols)
    got = received[:, local_members:].reshape(n_member, 3, local_members, own_cols)
    got = got.astype(jnp.float32)
    fac = ((got[:, 0] + got[:, 1]) + got[:, 2]).reshape(members, own_cols)
    j_iota = jnp.arange(members, dtype=jnp.int32)
    eye = (j_iota[:, None] == j_iota[None, :]).astype(jnp.bfloat16)
    ens_t = jnp.einsum("jtc,jk->tck", ens, eye, preferred_element_type=jnp.bfloat16)
    ens32 = ens_t.astype(jnp.float32)
    mean = jnp.sum(ens32, axis=2) / members
    anomaly = ((ens32 - mean[:, :, None]) * fac.T[None]).astype(jnp.bfloat16)
    mask = my_labels[None, :] == jnp.arange(n_slot, dtype=jnp.int32)[:, None]
    masked = jnp.where(mask[:, None, :, None], anomaly[None], jnp.zeros((), jnp.bfloat16))
    inc = jnp.einsum("rtcj,rjk->tck", masked, w_all, preferred_element_type=jnp.float32)
    inc = lax.reduce_precision(inc, exponent_bits=8, mantissa_bits=7)
    result_t = (mean[:, :, None] + inc).astype(jnp.bfloat16)
    result = jnp.einsum("kl,tcl->ktc", eye, result_t, preferred_element_type=jnp.bfloat16)
    result = result.reshape(n_member, local_members, tracers, own_cols)
    returned = lax.all_to_all(result, "member", split_axis=0, concat_axis=0, tiled=True)
    analysis = jnp.einsum("dkti,cdi->ktc", returned, perm_mat, preferred_element_type=jnp.bfloat16)

    local_index = obs_cols - me_space * columns
    obs_pos = jnp.take(position, local_index)
    obs_mat = (pos_iota[:, None] == obs_pos[None, :]).astype(jnp.bfloat16)
    obs_mat = obs_mat.reshape(n_member, own_cols, obs_cols.shape[0])
    picked = jnp.einsum("dkti,dio->kto", returned, obs_mat, preferred_element_type=jnp.float32)
    obs_analysis = jnp.einsum("t,kto->ko", extinction, picked, precision=lax.Precision.HIGHEST)
    return (analysis, obs_analysis)


def solution(mesh):
    in_specs = (
        P("member", None, "space"),
        P("member", None),
        P("space", None, None),
        P("space"),
        P(),
        P("space"),
    )
    out_specs = (P("member", None, "space"), P("member", "space"))
    return jax.shard_map(local, mesh=mesh, in_specs=in_specs, out_specs=out_specs, check_vma=False)
```

```python
import jax
import jax.numpy as jnp
from jax import lax
from jax.sharding import PartitionSpec as P


def _split3(x):
    hi = lax.reduce_precision(x, exponent_bits=8, mantissa_bits=7)
    r1 = x - hi
    mid = lax.reduce_precision(r1, exponent_bits=8, mantissa_bits=7)
    lo = r1 - mid
    return hi.astype(jnp.bfloat16), mid.astype(jnp.bfloat16), lo.astype(jnp.bfloat16)


def local(ensemble, inflation, weights, region_ids, extinction, obs_cols):
    n_space = lax.axis_size("space")
    n_member = lax.axis_size("member")
    local_members, tracers, columns = ensemble.shape
    members = local_members * n_member
    reg_count = weights.shape[0]
    all_regions = inflation.shape[1]
    groups_per_dev = n_space // n_member
    send_cols = columns // n_space
    own_cols = columns // n_member
    n_chip = n_space // 2
    chips_per_dev = groups_per_dev // 2
    n_slot = groups_per_dev * reg_count
    me_space = lax.axis_index("space")
    me_member = lax.axis_index("member")
    chip = me_space // 2
    core = me_space % 2

    ring = n_chip // 2
    pairs = [(0, ring // 2)] + [(b, ring - b) for b in range(1, ring // 2)]
    pairs = pairs + [(a + ring, b + ring) for a, b in pairs]
    owner_of = [0] * n_chip
    slot_of = [0] * n_chip
    for m, pair in enumerate(pairs):
        for a, off in enumerate(pair):
            owner_of[off] = m
            slot_of[off] = a
    own = []
    for a in range(chips_per_dev):
        perm = []
        for m in range(n_member):
            for s in range(n_space):
                src = 2 * ((s // 2 + pairs[m][a]) % n_chip) + s % 2
                perm.append((m * n_space + src, m * n_space + s))
        own.append(lax.ppermute(weights, ("member", "space"), perm))
    own = jnp.stack(own)
    sib_perm = [(m * n_space + s, m * n_space + (s ^ 1)) for m in range(n_member) for s in range(n_space)]
    sib = lax.ppermute(own, ("member", "space"), sib_perm)
    w_all = jnp.concatenate([own, sib], axis=0).reshape(n_slot, members, members)

    group = region_ids // reg_count
    offset = (group // 2 - chip) % n_chip
    dest = jnp.array(owner_of, jnp.int32)[offset]
    slot = (group % 2 != core).astype(jnp.int32) * chips_per_dev + jnp.array(slot_of, jnp.int32)[offset]
    group_hot = (group[:, None] == jnp.arange(n_space, dtype=jnp.int32)[None, :]).astype(jnp.int32)
    before = jnp.cumsum(group_hot, axis=0) - group_hot
    rank_in = jnp.sum(before * group_hot, axis=1)
    position = dest * own_cols + slot * send_cols + rank_in
    label = slot * reg_count + region_ids % reg_count
    pos_iota = jnp.arange(columns, dtype=jnp.int32)
    perm_hot = position[:, None] == pos_iota[None, :]
    perm_mat = perm_hot.astype(jnp.bfloat16).reshape(columns, n_member, own_cols)
    label_sorted = jnp.sum(jnp.where(perm_hot, label[:, None], 0), axis=0).reshape(n_member, own_cols)
    my_labels = lax.dynamic_index_in_dim(label_sorted, me_member, 0, keepdims=False)

    region_hot = (jnp.arange(all_regions, dtype=jnp.int32)[:, None] == region_ids[None, :]).astype(
        jnp.float32
    )
    factor = jnp.dot(inflation, region_hot, precision=lax.Precision.HIGHEST)
    fac_perm = jnp.einsum(
        "jc,cdi->dji", factor, perm_mat.astype(jnp.float32), precision=lax.Precision.HIGHEST
    )
    flat = tracers * own_cols
    main = jnp.einsum("jtc,cdi->djti", ensemble, perm_mat, preferred_element_type=jnp.bfloat16)
    main = main.reshape(n_member, local_members, flat)
    hi, mid, lo = _split3(fac_perm)
    spare = 128 - (3 * own_cols) % 128
    pad = jnp.zeros((n_member, local_members, spare), jnp.bfloat16)
    payload = jnp.concatenate([main, hi, mid, lo, pad], axis=2)

    received = lax.all_to_all(payload, "member", split_axis=0, concat_axis=0, tiled=True)
    received = received.reshape(members, payload.shape[2])
    ens32 = received[:, :flat].astype(jnp.float32)
    got = received[:, flat:].astype(jnp.float32)
    fac = (got[:, 0:own_cols] + got[:, own_cols:2 * own_cols]) + got[:, 2 * own_cols:3 * own_cols]
    lane_col = jnp.arange(flat, dtype=jnp.int32) % own_cols
    spread = (jnp.arange(own_cols, dtype=jnp.int32)[:, None] == lane_col[None, :]).astype(jnp.float32)
    fac_wide = jnp.dot(fac, spread, precision=lax.Precision.HIGHEST)
    mean = jnp.sum(ens32, axis=0) / members
    anomaly = ((ens32 - mean[None]) * fac_wide).astype(jnp.bfloat16)
    mask = my_labels[None, :] == jnp.arange(n_slot, dtype=jnp.int32)[:, None]
    mask = jnp.tile(mask, (1, tracers))
    masked = jnp.where(mask[:, None, :], anomaly[None], jnp.zeros((), jnp.bfloat16))
    inc = jnp.einsum("rjk,rjx->kx", w_all, masked, preferred_element_type=jnp.float32)
    inc = lax.reduce_precision(inc, exponent_bits=8, mantissa_bits=7)
    result = (mean[None] + inc).astype(jnp.bfloat16)
    result = result.reshape(n_member, local_members, flat)
    returned = lax.all_to_all(result, "member", split_axis=0, concat_axis=0, tiled=True)
    returned = returned.reshape(n_member, local_members, tracers, own_cols)
    analysis = jnp.einsum("dkti,cdi->ktc", returned, perm_mat, preferred_element_type=jnp.bfloat16)

    local_index = obs_cols - me_space * columns
    obs_pos = jnp.take(position, local_index)
    obs_mat = (pos_iota[:, None] == obs_pos[None, :]).astype(jnp.bfloat16)
    obs_mat = obs_mat.reshape(n_member, own_cols, obs_cols.shape[0])
    picked = jnp.einsum("dkti,dio->kto", returned, obs_mat, preferred_element_type=jnp.float32)
    obs_analysis = jnp.einsum("t,kto->ko", extinction, picked, precision=lax.Precision.HIGHEST)
    return (analysis, obs_analysis)


def solution(mesh):
    in_specs = (
        P("member", None, "space"),
        P("member", None),
        P("space", None, None),
        P("space"),
        P(),
        P("space"),
    )
    out_specs = (P("member", None, "space"), P("member", "space"))
    return jax.shard_map(local, mesh=mesh, in_specs=in_specs, out_specs=out_specs, check_vma=False)
```

```python
import jax
import jax.numpy as jnp
from jax import lax
from jax.sharding import PartitionSpec as P


def _split3(x):
    hi = lax.reduce_precision(x, exponent_bits=8, mantissa_bits=7)
    r1 = x - hi
    mid = lax.reduce_precision(r1, exponent_bits=8, mantissa_bits=7)
    lo = r1 - mid
    return hi.astype(jnp.bfloat16), mid.astype(jnp.bfloat16), lo.astype(jnp.bfloat16)


def local(ensemble, inflation, weights, region_ids, extinction, obs_cols):
    n_space = lax.axis_size("space")
    n_member = lax.axis_size("member")
    local_members, tracers, columns = ensemble.shape
    members = local_members * n_member
    reg_count = weights.shape[0]
    all_regions = inflation.shape[1]
    groups_per_dev = n_space // n_member
    send_cols = columns // n_space
    own_cols = columns // n_member
    n_chip = n_space // 2
    chips_per_dev = groups_per_dev // 2
    n_slot = groups_per_dev * reg_count
    me_space = lax.axis_index("space")
    me_member = lax.axis_index("member")
    chip = me_space // 2
    core = me_space % 2

    ring = n_chip // 2
    pairs = [(0, ring // 2)] + [(b, ring - b) for b in range(1, ring // 2)]
    pairs = pairs + [(a + ring, b + ring) for a, b in pairs]
    pairs_of = [pairs, [pairs[m ^ 2] for m in range(n_member)]]
    owner_of = [[0] * n_chip for _ in range(2)]
    slot_of = [[0] * n_chip for _ in range(2)]
    for par in range(2):
        for m, pair in enumerate(pairs_of[par]):
            for a, off in enumerate(pair):
                owner_of[par][off] = m
                slot_of[par][off] = a
    own = []
    for a in range(chips_per_dev):
        perm = []
        for m in range(n_member):
            for s in range(n_space):
                p = s // 2
                src = 2 * ((p + pairs_of[p % 2][m][a]) % n_chip) + s % 2
                perm.append((m * n_space + src, m * n_space + s))
        assert len({src for src, _ in perm}) == len(perm)
        own.append(lax.ppermute(weights, ("member", "space"), perm))
    own = jnp.stack(own)
    sib_perm = [(m * n_space + s, m * n_space + (s ^ 1)) for m in range(n_member) for s in range(n_space)]
    sib = lax.ppermute(own, ("member", "space"), sib_perm)
    w_all = jnp.concatenate([own, sib], axis=0).reshape(n_slot, members, members)

    group = region_ids // reg_count
    offset = (group // 2 - chip) % n_chip
    par = chip % 2
    dest = jnp.array(owner_of, jnp.int32)[par, offset]
    slot = (group % 2 != core).astype(jnp.int32) * chips_per_dev + jnp.array(slot_of, jnp.int32)[par, offset]
    group_hot = (group[:, None] == jnp.arange(n_space, dtype=jnp.int32)[None, :]).astype(jnp.int32)
    before = jnp.cumsum(group_hot, axis=0) - group_hot
    rank_in = jnp.sum(before * group_hot, axis=1)
    position = dest * own_cols + slot * send_cols + rank_in
    label = slot * reg_count + region_ids % reg_count
    pos_iota = jnp.arange(columns, dtype=jnp.int32)
    perm_hot = position[:, None] == pos_iota[None, :]
    perm_mat = perm_hot.astype(jnp.bfloat16).reshape(columns, n_member, own_cols)
    label_sorted = jnp.sum(jnp.where(perm_hot, label[:, None], 0), axis=0).reshape(n_member, own_cols)
    my_labels = lax.dynamic_index_in_dim(label_sorted, me_member, 0, keepdims=False)

    region_hot = (jnp.arange(all_regions, dtype=jnp.int32)[:, None] == region_ids[None, :]).astype(
        jnp.float32
    )
    factor = jnp.dot(inflation, region_hot, precision=lax.Precision.HIGHEST)
    fac_perm = jnp.einsum(
        "jc,cdi->dji", factor, perm_mat.astype(jnp.float32), precision=lax.Precision.HIGHEST
    )
    flat = tracers * own_cols
    main = jnp.einsum("jtc,cdi->djti", ensemble, perm_mat, preferred_element_type=jnp.bfloat16)
    main = main.reshape(n_member, local_members, flat)
    hi, mid, lo = _split3(fac_perm)
    spare = 128 - (3 * own_cols) % 128
    pad = jnp.zeros((n_member, local_members, spare), jnp.bfloat16)
    payload = jnp.concatenate([main, hi, mid, lo, pad], axis=2)

    received = lax.all_to_all(payload, "member", split_axis=0, concat_axis=0, tiled=True)
    received = received.reshape(members, payload.shape[2])
    ens32 = received[:, :flat].astype(jnp.float32)
    got = received[:, flat:].astype(jnp.float32)
    fac = (got[:, 0:own_cols] + got[:, own_cols:2 * own_cols]) + got[:, 2 * own_cols:3 * own_cols]
    lane_col = jnp.arange(flat, dtype=jnp.int32) % own_cols
    spread = (jnp.arange(own_cols, dtype=jnp.int32)[:, None] == lane_col[None, :]).astype(jnp.float32)
    fac_wide = jnp.dot(fac, spread, precision=lax.Precision.HIGHEST)
    mean = jnp.sum(ens32, axis=0) / members
    anomaly = ((ens32 - mean[None]) * fac_wide).astype(jnp.bfloat16)
    mask = my_labels[None, :] == jnp.arange(n_slot, dtype=jnp.int32)[:, None]
    mask = jnp.tile(mask, (1, tracers))
    masked = jnp.where(mask[:, None, :], anomaly[None], jnp.zeros((), jnp.bfloat16))
    inc = jnp.einsum("rjk,rjx->kx", w_all, masked, preferred_element_type=jnp.float32)
    inc = lax.reduce_precision(inc, exponent_bits=8, mantissa_bits=7)
    result = (mean[None] + inc).astype(jnp.bfloat16)
    result = result.reshape(n_member, local_members, flat)
    returned = lax.all_to_all(result, "member", split_axis=0, concat_axis=0, tiled=True)
    returned = returned.reshape(n_member, local_members, tracers, own_cols)
    analysis = jnp.einsum("dkti,cdi->ktc", returned, perm_mat, preferred_element_type=jnp.bfloat16)

    local_index = obs_cols - me_space * columns
    obs_pos = jnp.take(position, local_index)
    obs_mat = (pos_iota[:, None] == obs_pos[None, :]).astype(jnp.bfloat16)
    obs_mat = obs_mat.reshape(n_member, own_cols, obs_cols.shape[0])
    picked = jnp.einsum("dkti,dio->kto", returned, obs_mat, preferred_element_type=jnp.float32)
    obs_analysis = jnp.einsum("t,kto->ko", extinction, picked, precision=lax.Precision.HIGHEST)
    return (analysis, obs_analysis)


def solution(mesh):
    in_specs = (
        P("member", None, "space"),
        P("member", None),
        P("space", None, None),
        P("space"),
        P(),
        P("space"),
    )
    out_specs = (P("member", None, "space"), P("member", "space"))
    return jax.shard_map(local, mesh=mesh, in_specs=in_specs, out_specs=out_specs, check_vma=False)
```

```python
import jax
import numpy as np
import jax.numpy as jnp
from jax import lax
from jax.sharding import PartitionSpec as P


def _split3(x):
    hi = lax.reduce_precision(x, exponent_bits=8, mantissa_bits=7)
    r1 = x - hi
    mid = lax.reduce_precision(r1, exponent_bits=8, mantissa_bits=7)
    lo = r1 - mid
    return hi.astype(jnp.bfloat16), mid.astype(jnp.bfloat16), lo.astype(jnp.bfloat16)


def local(ensemble, inflation, weights, region_ids, extinction, obs_cols):
    n_space = lax.axis_size("space")
    n_member = lax.axis_size("member")
    local_members, tracers, columns = ensemble.shape
    members = local_members * n_member
    reg_count = weights.shape[0]
    all_regions = inflation.shape[1]
    groups_per_dev = n_space // n_member
    send_cols = columns // n_space
    own_cols = columns // n_member
    n_chip = n_space // 2
    chips_per_dev = groups_per_dev // 2
    n_slot = groups_per_dev * reg_count
    me_space = lax.axis_index("space")
    me_member = lax.axis_index("member")
    chip = me_space // 2
    core = me_space % 2

    ring = n_chip // 2
    pairs = [(0, ring // 2)] + [(b, ring - b) for b in range(1, ring // 2)]
    pairs = pairs + [(a + ring, b + ring) for a, b in pairs]
    pairs_of = [pairs, [pairs[m ^ 2] for m in range(n_member)]]
    owner_of = [[0] * n_chip for _ in range(2)]
    slot_of = [[0] * n_chip for _ in range(2)]
    for par in range(2):
        for m, pair in enumerate(pairs_of[par]):
            for a, off in enumerate(pair):
                owner_of[par][off] = m
                slot_of[par][off] = a
    own = []
    for a in range(chips_per_dev):
        perm = []
        for m in range(n_member):
            for s in range(n_space):
                p = s // 2
                src = 2 * ((p + pairs_of[p % 2][m][a]) % n_chip) + s % 2
                perm.append((m * n_space + src, m * n_space + s))
        assert len({src for src, _ in perm}) == len(perm)
        own.append(lax.ppermute(weights, ("member", "space"), perm))
    own = jnp.stack(own)
    sib_perm = [(m * n_space + s, m * n_space + (s ^ 1)) for m in range(n_member) for s in range(n_space)]
    sib = lax.ppermute(own, ("member", "space"), sib_perm)
    w_all = jnp.concatenate([own, sib], axis=0).reshape(n_slot, members, members)

    group = region_ids // reg_count
    offset = (group // 2 - chip) % n_chip
    par = chip % 2
    half_ring = ring // 2

    def owner_slot(o, p, xp):
        r = o % ring
        base = xp.where(r == half_ring, 0, xp.where(r < half_ring, r, ring - r))
        return xp.bitwise_xor(base + half_ring * (o // ring), 2 * p), (r >= half_ring).astype(xp.int32)

    for p_ in range(2):
        o_ = np.arange(n_chip)
        m_, a_ = owner_slot(o_, p_, np)
        assert list(m_) == owner_of[p_] and list(a_) == slot_of[p_]
    dest, slot_a = owner_slot(offset, par, jnp)
    slot = (group % 2 != core).astype(jnp.int32) * chips_per_dev + slot_a
    group_hot = (group[:, None] == jnp.arange(n_space, dtype=jnp.int32)[None, :]).astype(jnp.int32)
    before = jnp.cumsum(group_hot, axis=0) - group_hot
    rank_in = jnp.sum(before * group_hot, axis=1)
    position = dest * own_cols + slot * send_cols + rank_in
    label = slot * reg_count + region_ids % reg_count
    pos_iota = jnp.arange(columns, dtype=jnp.int32)
    perm_hot = position[:, None] == pos_iota[None, :]
    perm_mat = perm_hot.astype(jnp.bfloat16).reshape(columns, n_member, own_cols)
    label_sorted = jnp.sum(jnp.where(perm_hot, label[:, None], 0), axis=0).reshape(n_member, own_cols)
    my_labels = lax.dynamic_index_in_dim(label_sorted, me_member, 0, keepdims=False)

    region_hot = (jnp.arange(all_regions, dtype=jnp.int32)[:, None] == region_ids[None, :]).astype(
        jnp.float32
    )
    factor = jnp.dot(inflation, region_hot, precision=lax.Precision.HIGHEST)
    fac_perm = jnp.einsum(
        "jc,cdi->dji", factor, perm_mat.astype(jnp.float32), precision=lax.Precision.HIGHEST
    )
    flat = tracers * own_cols
    main = jnp.einsum("jtc,cdi->djti", ensemble, perm_mat, preferred_element_type=jnp.bfloat16)
    main = main.reshape(n_member, local_members, flat)
    hi, mid, lo = _split3(fac_perm)
    spare = 128 - (3 * own_cols) % 128
    pad = jnp.zeros((n_member, local_members, spare), jnp.bfloat16)
    payload = jnp.concatenate([main, hi, mid, lo, pad], axis=2)

    received = lax.all_to_all(payload, "member", split_axis=0, concat_axis=0, tiled=True)
    received = received.reshape(members, payload.shape[2])
    ens32 = received[:, :flat].astype(jnp.float32)
    got = received[:, flat:].astype(jnp.float32)
    fac = (got[:, 0:own_cols] + got[:, own_cols:2 * own_cols]) + got[:, 2 * own_cols:3 * own_cols]
    lane_col = jnp.arange(flat, dtype=jnp.int32) % own_cols
    spread = (jnp.arange(own_cols, dtype=jnp.int32)[:, None] == lane_col[None, :]).astype(jnp.float32)
    fac_wide = jnp.dot(fac, spread, precision=lax.Precision.HIGHEST)
    mean = jnp.sum(ens32, axis=0) / members
    anomaly = ((ens32 - mean[None]) * fac_wide).astype(jnp.bfloat16)
    mask = my_labels[None, :] == jnp.arange(n_slot, dtype=jnp.int32)[:, None]
    mask = jnp.tile(mask, (1, tracers))
    masked = jnp.where(mask[:, None, :], anomaly[None], jnp.zeros((), jnp.bfloat16))
    inc = jnp.einsum("rjk,rjx->kx", w_all, masked, preferred_element_type=jnp.float32)
    inc = lax.reduce_precision(inc, exponent_bits=8, mantissa_bits=7)
    result = (mean[None] + inc).astype(jnp.bfloat16)
    result = result.reshape(n_member, local_members, flat)
    returned = lax.all_to_all(result, "member", split_axis=0, concat_axis=0, tiled=True)
    returned = returned.reshape(n_member, local_members, tracers, own_cols)
    analysis = jnp.einsum("dkti,cdi->ktc", returned, perm_mat, preferred_element_type=jnp.bfloat16)

    local_index = obs_cols - me_space * columns
    obs_pos = jnp.take(position, local_index)
    obs_mat = (pos_iota[:, None] == obs_pos[None, :]).astype(jnp.bfloat16)
    obs_mat = obs_mat.reshape(n_member, own_cols, obs_cols.shape[0])
    picked = jnp.einsum("dkti,dio->kto", returned, obs_mat, preferred_element_type=jnp.float32)
    obs_analysis = jnp.einsum("t,kto->ko", extinction, picked, precision=lax.Precision.HIGHEST)
    return (analysis, obs_analysis)


def solution(mesh):
    in_specs = (
        P("member", None, "space"),
        P("member", None),
        P("space", None, None),
        P("space"),
        P(),
        P("space"),
    )
    out_specs = (P("member", None, "space"), P("member", "space"))
    return jax.shard_map(local, mesh=mesh, in_specs=in_specs, out_specs=out_specs, check_vma=False)
```

```python
import jax
import numpy as np
import jax.numpy as jnp
from jax import lax
from jax.sharding import PartitionSpec as P


def _split3(x):
    hi = lax.reduce_precision(x, exponent_bits=8, mantissa_bits=7)
    r1 = x - hi
    mid = lax.reduce_precision(r1, exponent_bits=8, mantissa_bits=7)
    lo = r1 - mid
    return hi.astype(jnp.bfloat16), mid.astype(jnp.bfloat16), lo.astype(jnp.bfloat16)


def local(ensemble, inflation, weights, region_ids, extinction, obs_cols):
    n_space = lax.axis_size("space")
    n_member = lax.axis_size("member")
    local_members, tracers, columns = ensemble.shape
    members = local_members * n_member
    reg_count = weights.shape[0]
    all_regions = inflation.shape[1]
    groups_per_dev = n_space // n_member
    send_cols = columns // n_space
    own_cols = columns // n_member
    n_chip = n_space // 2
    chips_per_dev = groups_per_dev // 2
    n_slot = groups_per_dev * reg_count
    me_space = lax.axis_index("space")
    me_member = lax.axis_index("member")
    chip = me_space // 2
    core = me_space % 2

    ring = n_chip // 2
    pairs = [(0, ring // 2)] + [(b, ring - b) for b in range(1, ring // 2)]
    pairs = pairs + [(a + ring, b + ring) for a, b in pairs]
    pairs_of = [pairs, [pairs[m ^ 2] for m in range(n_member)]]
    owner_of = [[0] * n_chip for _ in range(2)]
    slot_of = [[0] * n_chip for _ in range(2)]
    for par in range(2):
        for m, pair in enumerate(pairs_of[par]):
            for a, off in enumerate(pair):
                owner_of[par][off] = m
                slot_of[par][off] = a
    own = []
    for a in range(chips_per_dev):
        perm = []
        for m in range(n_member):
            for s in range(n_space):
                p = s // 2
                src = 2 * ((p + pairs_of[p % 2][m][a]) % n_chip) + s % 2
                perm.append((m * n_space + src, m * n_space + s))
        assert len({src for src, _ in perm}) == len(perm)
        own.append(lax.ppermute(weights, ("member", "space"), perm))
    sib_perm = [(m * n_space + s, m * n_space + (s ^ 1)) for m in range(n_member) for s in range(n_space)]
    sib = [lax.ppermute(w, ("member", "space"), sib_perm) for w in own]
    w_blocks = own + sib

    group = region_ids // reg_count
    offset = (group // 2 - chip) % n_chip
    par = chip % 2
    half_ring = ring // 2

    def owner_slot(o, p, xp):
        r = o % ring
        base = xp.where(r == half_ring, 0, xp.where(r < half_ring, r, ring - r))
        return xp.bitwise_xor(base + half_ring * (o // ring), 2 * p), (r >= half_ring).astype(xp.int32)

    for p_ in range(2):
        o_ = np.arange(n_chip)
        m_, a_ = owner_slot(o_, p_, np)
        assert list(m_) == owner_of[p_] and list(a_) == slot_of[p_]
    dest, slot_a = owner_slot(offset, par, jnp)
    slot = (group % 2 != core).astype(jnp.int32) * chips_per_dev + slot_a
    group_hot = (group[:, None] == jnp.arange(n_space, dtype=jnp.int32)[None, :]).astype(jnp.int32)
    before = jnp.cumsum(group_hot, axis=0) - group_hot
    rank_in = jnp.sum(before * group_hot, axis=1)
    position = dest * own_cols + slot * send_cols + rank_in
    label = slot * reg_count + region_ids % reg_count
    pos_iota = jnp.arange(columns, dtype=jnp.int32)
    perm_hot = position[:, None] == pos_iota[None, :]
    perm_mat = perm_hot.astype(jnp.bfloat16).reshape(columns, n_member, own_cols)
    label_sorted = jnp.sum(jnp.where(perm_hot, label[:, None], 0), axis=0).reshape(n_member, own_cols)
    my_labels = lax.dynamic_index_in_dim(label_sorted, me_member, 0, keepdims=False)

    region_hot = (jnp.arange(all_regions, dtype=jnp.int32)[:, None] == region_ids[None, :]).astype(
        jnp.float32
    )
    factor = jnp.dot(inflation, region_hot, precision=lax.Precision.HIGHEST)
    fac_perm = jnp.einsum(
        "jc,cdi->dji", factor, perm_mat.astype(jnp.float32), precision=lax.Precision.HIGHEST
    )
    flat = tracers * own_cols
    main = jnp.einsum("jtc,cdi->djti", ensemble, perm_mat, preferred_element_type=jnp.bfloat16)
    main = main.reshape(n_member, local_members, flat)
    hi, mid, lo = _split3(fac_perm)
    spare = 128 - (3 * own_cols) % 128
    pad = jnp.zeros((n_member, local_members, spare), jnp.bfloat16)
    payload = jnp.concatenate([main, hi, mid, lo, pad], axis=2)

    received = lax.all_to_all(payload, "member", split_axis=0, concat_axis=0, tiled=True)
    received = received.reshape(members, payload.shape[2])
    ens32 = received[:, :flat].astype(jnp.float32)
    got = received[:, flat:].astype(jnp.float32)
    fac = (got[:, 0:own_cols] + got[:, own_cols:2 * own_cols]) + got[:, 2 * own_cols:3 * own_cols]
    lane_col = jnp.arange(flat, dtype=jnp.int32) % own_cols
    spread = (jnp.arange(own_cols, dtype=jnp.int32)[:, None] == lane_col[None, :]).astype(jnp.float32)
    fac_wide = jnp.dot(fac, spread, precision=lax.Precision.HIGHEST)
    mean = jnp.sum(ens32, axis=0) / members
    anomaly = ((ens32 - mean[None]) * fac_wide).astype(jnp.bfloat16)
    mask = my_labels[None, :] == jnp.arange(n_slot, dtype=jnp.int32)[:, None]
    mask = jnp.tile(mask, (1, tracers))
    masked = jnp.where(mask[:, None, :], anomaly[None], jnp.zeros((), jnp.bfloat16))
    inc = None
    for b, w in enumerate(w_blocks):
        part = jnp.einsum(
            "rjk,rjx->kx", w, masked[b * reg_count:(b + 1) * reg_count],
            preferred_element_type=jnp.float32,
        )
        inc = part if inc is None else inc + part
    inc = lax.reduce_precision(inc, exponent_bits=8, mantissa_bits=7)
    result = (mean[None] + inc).astype(jnp.bfloat16)
    result = result.reshape(n_member, local_members, flat)
    returned = lax.all_to_all(result, "member", split_axis=0, concat_axis=0, tiled=True)
    returned = returned.reshape(n_member, local_members, tracers, own_cols)
    analysis = jnp.einsum("dkti,cdi->ktc", returned, perm_mat, preferred_element_type=jnp.bfloat16)

    local_index = obs_cols - me_space * columns
    obs_pos = jnp.take(position, local_index)
    obs_mat = (pos_iota[:, None] == obs_pos[None, :]).astype(jnp.bfloat16)
    obs_mat = obs_mat.reshape(n_member, own_cols, obs_cols.shape[0])
    picked = jnp.einsum("dkti,dio->kto", returned, obs_mat, preferred_element_type=jnp.float32)
    obs_analysis = jnp.einsum("t,kto->ko", extinction, picked, precision=lax.Precision.HIGHEST)
    return (analysis, obs_analysis)


def solution(mesh):
    in_specs = (
        P("member", None, "space"),
        P("member", None),
        P("space", None, None),
        P("space"),
        P(),
        P("space"),
    )
    out_specs = (P("member", None, "space"), P("member", "space"))
    return jax.shard_map(local, mesh=mesh, in_specs=in_specs, out_specs=out_specs, check_vma=False)
```

```python
import jax
import numpy as np
import jax.numpy as jnp
from jax import lax
from jax.sharding import PartitionSpec as P


def _split3(x):
    hi = lax.reduce_precision(x, exponent_bits=8, mantissa_bits=7)
    r1 = x - hi
    mid = lax.reduce_precision(r1, exponent_bits=8, mantissa_bits=7)
    lo = r1 - mid
    return hi.astype(jnp.bfloat16), mid.astype(jnp.bfloat16), lo.astype(jnp.bfloat16)


def local(ensemble, inflation, weights, region_ids, extinction, obs_cols):
    n_space = lax.axis_size("space")
    n_member = lax.axis_size("member")
    local_members, tracers, columns = ensemble.shape
    members = local_members * n_member
    reg_count = weights.shape[0]
    all_regions = inflation.shape[1]
    groups_per_dev = n_space // n_member
    send_cols = columns // n_space
    own_cols = columns // n_member
    n_chip = n_space // 2
    chips_per_dev = groups_per_dev // 2
    n_slot = groups_per_dev * reg_count
    me_space = lax.axis_index("space")
    me_member = lax.axis_index("member")
    chip = me_space // 2
    core = me_space % 2

    ring = n_chip // 2
    pairs = [(0, ring // 2)] + [(b, ring - b) for b in range(1, ring // 2)]
    pairs = pairs + [(a + ring, b + ring) for a, b in pairs]
    pairs_of = [pairs, [pairs[m ^ 2] for m in range(n_member)]]
    owner_of = [[0] * n_chip for _ in range(2)]
    slot_of = [[0] * n_chip for _ in range(2)]
    for par in range(2):
        for m, pair in enumerate(pairs_of[par]):
            for a, off in enumerate(pair):
                owner_of[par][off] = m
                slot_of[par][off] = a
    own = []
    for a in range(chips_per_dev):
        perm = []
        for m in range(n_member):
            for s in range(n_space):
                p = s // 2
                src = 2 * ((p + pairs_of[p % 2][m][a]) % n_chip) + s % 2
                perm.append((m * n_space + src, m * n_space + s))
        assert len({src for src, _ in perm}) == len(perm)
        own.append(lax.ppermute(weights, ("member", "space"), perm))
    own = jnp.stack(own)
    sib_perm = [(m * n_space + s, m * n_space + (s ^ 1)) for m in range(n_member) for s in range(n_space)]
    sib = lax.ppermute(own, ("member", "space"), sib_perm)
    w_all = jnp.concatenate([own, sib], axis=0).reshape(n_slot, members, members)

    group = region_ids // reg_count
    offset = (group // 2 - chip) % n_chip
    par = chip % 2
    half_ring = ring // 2

    def owner_slot(o, p, xp):
        r = o % ring
        base = xp.where(r == half_ring, 0, xp.where(r < half_ring, r, ring - r))
        return xp.bitwise_xor(base + half_ring * (o // ring), 2 * p), (r >= half_ring).astype(xp.int32)

    for p_ in range(2):
        o_ = np.arange(n_chip)
        m_, a_ = owner_slot(o_, p_, np)
        assert list(m_) == owner_of[p_] and list(a_) == slot_of[p_]
    dest, slot_a = owner_slot(offset, par, jnp)
    slot = (group % 2 != core).astype(jnp.int32) * chips_per_dev + slot_a
    group_hot = (group[:, None] == jnp.arange(n_space, dtype=jnp.int32)[None, :]).astype(jnp.int32)
    before = jnp.cumsum(group_hot, axis=0) - group_hot
    rank_in = jnp.sum(before * group_hot, axis=1)
    position = dest * own_cols + slot * send_cols + rank_in
    label = slot * reg_count + region_ids % reg_count
    pos_iota = jnp.arange(columns, dtype=jnp.int32)
    perm_hot = position[:, None] == pos_iota[None, :]
    perm_mat = perm_hot.astype(jnp.bfloat16).reshape(columns, n_member, own_cols)
    label_sorted = jnp.sum(jnp.where(perm_hot, label[:, None], 0), axis=0).reshape(n_member, own_cols)
    my_labels = lax.dynamic_index_in_dim(label_sorted, me_member, 0, keepdims=False)

    region_hot = (jnp.arange(all_regions, dtype=jnp.int32)[:, None] == region_ids[None, :]).astype(
        jnp.float32
    )
    factor = jnp.dot(inflation, region_hot, precision=lax.Precision.HIGHEST)
    fac_perm = jnp.einsum(
        "jc,cdi->dji", factor, perm_mat.astype(jnp.float32), precision=lax.Precision.HIGHEST
    )
    flat = tracers * own_cols
    main = jnp.einsum("jtc,cdi->djti", ensemble, perm_mat, preferred_element_type=jnp.bfloat16)
    main = main.reshape(n_member, local_members, flat)
    hi, mid, lo = _split3(fac_perm)
    spare = 128 - (3 * own_cols) % 128
    pad = jnp.zeros((n_member, local_members, spare), jnp.bfloat16)
    payload = jnp.concatenate([main, hi, mid, lo, pad], axis=2)

    received = lax.all_to_all(payload, "member", split_axis=0, concat_axis=0, tiled=True)
    received = received.reshape(members, payload.shape[2])
    ens32 = received[:, :flat].astype(jnp.float32)
    got = received[:, flat:].astype(jnp.float32)
    fac = (got[:, 0:own_cols] + got[:, own_cols:2 * own_cols]) + got[:, 2 * own_cols:3 * own_cols]
    lane_col = jnp.arange(flat, dtype=jnp.int32) % own_cols
    spread = (jnp.arange(own_cols, dtype=jnp.int32)[:, None] == lane_col[None, :]).astype(jnp.float32)
    fac_wide = jnp.dot(fac, spread, precision=lax.Precision.HIGHEST)
    mean = jnp.sum(ens32, axis=0) / members
    anomaly = ((ens32 - mean[None]) * fac_wide).astype(jnp.bfloat16)
    mask = my_labels[None, :] == jnp.arange(n_slot, dtype=jnp.int32)[:, None]
    mask = jnp.tile(mask, (1, tracers))
    masked = jnp.where(mask[:, None, :], anomaly[None], jnp.zeros((), jnp.bfloat16))
    inc = jnp.einsum("rjk,rjx->kx", w_all, masked, preferred_element_type=jnp.float32)
    inc = lax.reduce_precision(inc, exponent_bits=8, mantissa_bits=7)
    result = (mean[None] + inc).astype(jnp.bfloat16)
    result = result.reshape(n_member, local_members, flat)
    local_index = obs_cols - me_space * columns
    obs_pos = jnp.take(position, local_index)
    obs_mat = (pos_iota[:, None] == obs_pos[None, :]).astype(jnp.bfloat16)
    obs_mat = obs_mat.reshape(n_member, own_cols, obs_cols.shape[0])
    chunk = local_members // 2
    pieces_a, pieces_o = [], []
    for part in range(2):
        sent = result[:, part * chunk:(part + 1) * chunk]
        back = lax.all_to_all(sent, "member", split_axis=0, concat_axis=0, tiled=True)
        back = back.reshape(n_member, chunk, tracers, own_cols)
        pieces_a.append(
            jnp.einsum("dkti,cdi->ktc", back, perm_mat, preferred_element_type=jnp.bfloat16)
        )
        pieces_o.append(
            jnp.einsum("dkti,dio->kto", back, obs_mat, preferred_element_type=jnp.float32)
        )
    analysis = jnp.concatenate(pieces_a, axis=0)
    picked = jnp.concatenate(pieces_o, axis=0)
    obs_analysis = jnp.einsum("t,kto->ko", extinction, picked, precision=lax.Precision.HIGHEST)
    return (analysis, obs_analysis)


def solution(mesh):
    in_specs = (
        P("member", None, "space"),
        P("member", None),
        P("space", None, None),
        P("space"),
        P(),
        P("space"),
    )
    out_specs = (P("member", None, "space"), P("member", "space"))
    return jax.shard_map(local, mesh=mesh, in_specs=in_specs, out_specs=out_specs, check_vma=False)
```

```python
import jax
import numpy as np
import jax.numpy as jnp
from jax import lax
from jax.sharding import PartitionSpec as P


def _split3(x):
    hi = lax.reduce_precision(x, exponent_bits=8, mantissa_bits=7)
    r1 = x - hi
    mid = lax.reduce_precision(r1, exponent_bits=8, mantissa_bits=7)
    lo = r1 - mid
    return hi.astype(jnp.bfloat16), mid.astype(jnp.bfloat16), lo.astype(jnp.bfloat16)


def local(ensemble, inflation, weights, region_ids, extinction, obs_cols):
    n_space = lax.axis_size("space")
    n_member = lax.axis_size("member")
    local_members, tracers, columns = ensemble.shape
    members = local_members * n_member
    reg_count = weights.shape[0]
    all_regions = inflation.shape[1]
    groups_per_dev = n_space // n_member
    send_cols = columns // n_space
    own_cols = columns // n_member
    n_chip = n_space // 2
    chips_per_dev = groups_per_dev // 2
    n_slot = groups_per_dev * reg_count
    me_space = lax.axis_index("space")
    me_member = lax.axis_index("member")
    chip = me_space // 2
    core = me_space % 2

    ring = n_chip // 2
    pairs = [(0, ring // 2)] + [(b, ring - b) for b in range(1, ring // 2)]
    pairs = pairs + [(a + ring, b + ring) for a, b in pairs]
    pairs_of = [pairs, [pairs[m ^ 2] for m in range(n_member)]]
    owner_of = [[0] * n_chip for _ in range(2)]
    slot_of = [[0] * n_chip for _ in range(2)]
    for par in range(2):
        for m, pair in enumerate(pairs_of[par]):
            for a, off in enumerate(pair):
                owner_of[par][off] = m
                slot_of[par][off] = a
    own = []
    for a in range(chips_per_dev):
        perm = []
        for m in range(n_member):
            for s in range(n_space):
                p = s // 2
                src = 2 * ((p + pairs_of[p % 2][m][a]) % n_chip) + s % 2
                perm.append((m * n_space + src, m * n_space + s))
        assert len({src for src, _ in perm}) == len(perm)
        own.append(lax.ppermute(weights, ("member", "space"), perm))
    sib_perm = [(m * n_space + s, m * n_space + (s ^ 1)) for m in range(n_member) for s in range(n_space)]

    group = region_ids // reg_count
    offset = (group // 2 - chip) % n_chip
    par = chip % 2
    half_ring = ring // 2

    def owner_slot(o, p, xp):
        r = o % ring
        base = xp.where(r == half_ring, 0, xp.where(r < half_ring, r, ring - r))
        return xp.bitwise_xor(base + half_ring * (o // ring), 2 * p), (r >= half_ring).astype(xp.int32)

    for p_ in range(2):
        o_ = np.arange(n_chip)
        m_, a_ = owner_slot(o_, p_, np)
        assert list(m_) == owner_of[p_] and list(a_) == slot_of[p_]
    dest, slot_a = owner_slot(offset, par, jnp)
    slot = (group % 2 != core).astype(jnp.int32) * chips_per_dev + slot_a
    group_hot = (group[:, None] == jnp.arange(n_space, dtype=jnp.int32)[None, :]).astype(jnp.int32)
    before = jnp.cumsum(group_hot, axis=0) - group_hot
    rank_in = jnp.sum(before * group_hot, axis=1)
    position = dest * own_cols + slot * send_cols + rank_in
    label = slot * reg_count + region_ids % reg_count
    pos_iota = jnp.arange(columns, dtype=jnp.int32)
    perm_hot = position[:, None] == pos_iota[None, :]
    perm_mat = perm_hot.astype(jnp.bfloat16).reshape(columns, n_member, own_cols)
    label_sorted = jnp.sum(jnp.where(perm_hot, label[:, None], 0), axis=0).reshape(n_member, own_cols)
    my_labels = lax.dynamic_index_in_dim(label_sorted, me_member, 0, keepdims=False)

    region_hot = (jnp.arange(all_regions, dtype=jnp.int32)[:, None] == region_ids[None, :]).astype(
        jnp.float32
    )
    factor = jnp.dot(inflation, region_hot, precision=lax.Precision.HIGHEST)
    fac_perm = jnp.einsum(
        "jc,cdi->dji", factor, perm_mat.astype(jnp.float32), precision=lax.Precision.HIGHEST
    )
    flat = tracers * own_cols
    main = jnp.einsum("jtc,cdi->djti", ensemble, perm_mat, preferred_element_type=jnp.bfloat16)
    main = main.reshape(n_member, local_members, flat)
    hi, mid, lo = _split3(fac_perm)
    spare = 128 - (3 * own_cols) % 128
    pad = jnp.zeros((n_member, local_members, spare), jnp.bfloat16)
    payload = jnp.concatenate([main, hi, mid, lo, pad], axis=2)

    payload, near = lax.optimization_barrier((payload, own[0]))
    own = jnp.stack([near] + own[1:])
    sib = lax.ppermute(own, ("member", "space"), sib_perm)
    w_all = jnp.concatenate([own, sib], axis=0).reshape(n_slot, members, members)
    received = lax.all_to_all(payload, "member", split_axis=0, concat_axis=0, tiled=True)
    received = received.reshape(members, payload.shape[2])
    ens32 = received[:, :flat].astype(jnp.float32)
    got = received[:, flat:].astype(jnp.float32)
    fac = (got[:, 0:own_cols] + got[:, own_cols:2 * own_cols]) + got[:, 2 * own_cols:3 * own_cols]
    lane_col = jnp.arange(flat, dtype=jnp.int32) % own_cols
    spread = (jnp.arange(own_cols, dtype=jnp.int32)[:, None] == lane_col[None, :]).astype(jnp.float32)
    fac_wide = jnp.dot(fac, spread, precision=lax.Precision.HIGHEST)
    mean = jnp.sum(ens32, axis=0) / members
    anomaly = ((ens32 - mean[None]) * fac_wide).astype(jnp.bfloat16)
    mask = my_labels[None, :] == jnp.arange(n_slot, dtype=jnp.int32)[:, None]
    mask = jnp.tile(mask, (1, tracers))
    masked = jnp.where(mask[:, None, :], anomaly[None], jnp.zeros((), jnp.bfloat16))
    inc = jnp.einsum("rjk,rjx->kx", w_all, masked, preferred_element_type=jnp.float32)
    inc = lax.reduce_precision(inc, exponent_bits=8, mantissa_bits=7)
    result = (mean[None] + inc).astype(jnp.bfloat16)
    result = result.reshape(n_member, local_members, flat)
    returned = lax.all_to_all(result, "member", split_axis=0, concat_axis=0, tiled=True)
    returned = returned.reshape(n_member, local_members, tracers, own_cols)
    analysis = jnp.einsum("dkti,cdi->ktc", returned, perm_mat, preferred_element_type=jnp.bfloat16)

    local_index = obs_cols - me_space * columns
    obs_pos = jnp.take(position, local_index)
    obs_mat = (pos_iota[:, None] == obs_pos[None, :]).astype(jnp.bfloat16)
    obs_mat = obs_mat.reshape(n_member, own_cols, obs_cols.shape[0])
    picked = jnp.einsum("dkti,dio->kto", returned, obs_mat, preferred_element_type=jnp.float32)
    obs_analysis = jnp.einsum("t,kto->ko", extinction, picked, precision=lax.Precision.HIGHEST)
    return (analysis, obs_analysis)


def solution(mesh):
    in_specs = (
        P("member", None, "space"),
        P("member", None),
        P("space", None, None),
        P("space"),
        P(),
        P("space"),
    )
    out_specs = (P("member", None, "space"), P("member", "space"))
    return jax.shard_map(local, mesh=mesh, in_specs=in_specs, out_specs=out_specs, check_vma=False)
```

```python
import jax
import numpy as np
import jax.numpy as jnp
from jax import lax
from jax.sharding import PartitionSpec as P


def _split3(x):
    hi = lax.reduce_precision(x, exponent_bits=8, mantissa_bits=7)
    r1 = x - hi
    mid = lax.reduce_precision(r1, exponent_bits=8, mantissa_bits=7)
    lo = r1 - mid
    return hi.astype(jnp.bfloat16), mid.astype(jnp.bfloat16), lo.astype(jnp.bfloat16)


def local(ensemble, inflation, weights, region_ids, extinction, obs_cols):
    n_space = lax.axis_size("space")
    n_member = lax.axis_size("member")
    local_members, tracers, columns = ensemble.shape
    members = local_members * n_member
    reg_count = weights.shape[0]
    all_regions = inflation.shape[1]
    groups_per_dev = n_space // n_member
    send_cols = columns // n_space
    own_cols = columns // n_member
    n_chip = n_space // 2
    chips_per_dev = groups_per_dev // 2
    n_slot = groups_per_dev * reg_count
    me_space = lax.axis_index("space")
    me_member = lax.axis_index("member")
    chip = me_space // 2
    core = me_space % 2

    ring = n_chip // 2
    pairs = [(0, ring // 2)] + [(b, ring - b) for b in range(1, ring // 2)]
    pairs = pairs + [(a + ring, b + ring) for a, b in pairs]
    pairs_of = [pairs, [pairs[m ^ 2] for m in range(n_member)]]
    owner_of = [[0] * n_chip for _ in range(2)]
    slot_of = [[0] * n_chip for _ in range(2)]
    for par in range(2):
        for m, pair in enumerate(pairs_of[par]):
            for a, off in enumerate(pair):
                owner_of[par][off] = m
                slot_of[par][off] = a
    own = []
    for a in range(chips_per_dev):
        perm = []
        for m in range(n_member):
            for s in range(n_space):
                p = s // 2
                src = 2 * ((p + pairs_of[p % 2][m][a]) % n_chip) + s % 2
                perm.append((m * n_space + src, m * n_space + s))
        assert len({src for src, _ in perm}) == len(perm)
        if a == 0:
            half_reg = reg_count // 2
            first = lax.ppermute(weights[:half_reg], ("member", "space"), perm)
            rest = lax.ppermute(weights[half_reg:], ("member", "space"), perm)
            own.append(None)
        else:
            own.append(lax.ppermute(weights, ("member", "space"), perm))
    sib_perm = [(m * n_space + s, m * n_space + (s ^ 1)) for m in range(n_member) for s in range(n_space)]

    group = region_ids // reg_count
    offset = (group // 2 - chip) % n_chip
    par = chip % 2
    half_ring = ring // 2

    def owner_slot(o, p, xp):
        r = o % ring
        base = xp.where(r == half_ring, 0, xp.where(r < half_ring, r, ring - r))
        return xp.bitwise_xor(base + half_ring * (o // ring), 2 * p), (r >= half_ring).astype(xp.int32)

    for p_ in range(2):
        o_ = np.arange(n_chip)
        m_, a_ = owner_slot(o_, p_, np)
        assert list(m_) == owner_of[p_] and list(a_) == slot_of[p_]
    dest, slot_a = owner_slot(offset, par, jnp)
    slot = (group % 2 != core).astype(jnp.int32) * chips_per_dev + slot_a
    group_hot = (group[:, None] == jnp.arange(n_space, dtype=jnp.int32)[None, :]).astype(jnp.int32)
    before = jnp.cumsum(group_hot, axis=0) - group_hot
    rank_in = jnp.sum(before * group_hot, axis=1)
    position = dest * own_cols + slot * send_cols + rank_in
    label = slot * reg_count + region_ids % reg_count
    pos_iota = jnp.arange(columns, dtype=jnp.int32)
    perm_hot = position[:, None] == pos_iota[None, :]
    perm_mat = perm_hot.astype(jnp.bfloat16).reshape(columns, n_member, own_cols)
    label_sorted = jnp.sum(jnp.where(perm_hot, label[:, None], 0), axis=0).reshape(n_member, own_cols)
    my_labels = lax.dynamic_index_in_dim(label_sorted, me_member, 0, keepdims=False)

    region_hot = (jnp.arange(all_regions, dtype=jnp.int32)[:, None] == region_ids[None, :]).astype(
        jnp.float32
    )
    factor = jnp.dot(inflation, region_hot, precision=lax.Precision.HIGHEST)
    fac_perm = jnp.einsum(
        "jc,cdi->dji", factor, perm_mat.astype(jnp.float32), precision=lax.Precision.HIGHEST
    )
    flat = tracers * own_cols
    main = jnp.einsum("jtc,cdi->djti", ensemble, perm_mat, preferred_element_type=jnp.bfloat16)
    main = main.reshape(n_member, local_members, flat)
    hi, mid, lo = _split3(fac_perm)
    spare = 128 - (3 * own_cols) % 128
    pad = jnp.zeros((n_member, local_members, spare), jnp.bfloat16)
    payload = jnp.concatenate([main, hi, mid, lo, pad], axis=2)

    payload, first = lax.optimization_barrier((payload, first))
    own = jnp.stack([jnp.concatenate([first, rest], axis=0)] + own[1:])
    sib = lax.ppermute(own, ("member", "space"), sib_perm)
    w_all = jnp.concatenate([own, sib], axis=0).reshape(n_slot, members, members)
    received = lax.all_to_all(payload, "member", split_axis=0, concat_axis=0, tiled=True)
    received = received.reshape(members, payload.shape[2])
    ens32 = received[:, :flat].astype(jnp.float32)
    got = received[:, flat:].astype(jnp.float32)
    fac = (got[:, 0:own_cols] + got[:, own_cols:2 * own_cols]) + got[:, 2 * own_cols:3 * own_cols]
    lane_col = jnp.arange(flat, dtype=jnp.int32) % own_cols
    spread = (jnp.arange(own_cols, dtype=jnp.int32)[:, None] == lane_col[None, :]).astype(jnp.float32)
    fac_wide = jnp.dot(fac, spread, precision=lax.Precision.HIGHEST)
    mean = jnp.sum(ens32, axis=0) / members
    anomaly = ((ens32 - mean[None]) * fac_wide).astype(jnp.bfloat16)
    mask = my_labels[None, :] == jnp.arange(n_slot, dtype=jnp.int32)[:, None]
    mask = jnp.tile(mask, (1, tracers))
    masked = jnp.where(mask[:, None, :], anomaly[None], jnp.zeros((), jnp.bfloat16))
    inc = jnp.einsum("rjk,rjx->kx", w_all, masked, preferred_element_type=jnp.float32)
    inc = lax.reduce_precision(inc, exponent_bits=8, mantissa_bits=7)
    result = (mean[None] + inc).astype(jnp.bfloat16)
    result = result.reshape(n_member, local_members, flat)
    returned = lax.all_to_all(result, "member", split_axis=0, concat_axis=0, tiled=True)
    returned = returned.reshape(n_member, local_members, tracers, own_cols)
    analysis = jnp.einsum("dkti,cdi->ktc", returned, perm_mat, preferred_element_type=jnp.bfloat16)

    local_index = obs_cols - me_space * columns
    obs_pos = jnp.take(position, local_index)
    obs_mat = (pos_iota[:, None] == obs_pos[None, :]).astype(jnp.bfloat16)
    obs_mat = obs_mat.reshape(n_member, own_cols, obs_cols.shape[0])
    picked = jnp.einsum("dkti,dio->kto", returned, obs_mat, preferred_element_type=jnp.float32)
    obs_analysis = jnp.einsum("t,kto->ko", extinction, picked, precision=lax.Precision.HIGHEST)
    return (analysis, obs_analysis)


def solution(mesh):
    in_specs = (
        P("member", None, "space"),
        P("member", None),
        P("space", None, None),
        P("space"),
        P(),
        P("space"),
    )
    out_specs = (P("member", None, "space"), P("member", "space"))
    return jax.shard_map(local, mesh=mesh, in_specs=in_specs, out_specs=out_specs, check_vma=False)
```

```python
import jax
import numpy as np
import jax.numpy as jnp
from jax import lax
from jax.sharding import PartitionSpec as P


def _split3(x):
    hi = lax.reduce_precision(x, exponent_bits=8, mantissa_bits=7)
    r1 = x - hi
    mid = lax.reduce_precision(r1, exponent_bits=8, mantissa_bits=7)
    lo = r1 - mid
    return hi.astype(jnp.bfloat16), mid.astype(jnp.bfloat16), lo.astype(jnp.bfloat16)


def local(ensemble, inflation, weights, region_ids, extinction, obs_cols):
    n_space = lax.axis_size("space")
    n_member = lax.axis_size("member")
    local_members, tracers, columns = ensemble.shape
    members = local_members * n_member
    reg_count = weights.shape[0]
    all_regions = inflation.shape[1]
    groups_per_dev = n_space // n_member
    send_cols = columns // n_space
    own_cols = columns // n_member
    n_chip = n_space // 2
    chips_per_dev = groups_per_dev // 2
    n_slot = groups_per_dev * reg_count
    me_space = lax.axis_index("space")
    me_member = lax.axis_index("member")
    chip = me_space // 2
    core = me_space % 2

    ring = n_chip // 2
    pairs = [(0, ring // 2)] + [(b, ring - b) for b in range(1, ring // 2)]
    pairs = pairs + [(a + ring, b + ring) for a, b in pairs]
    pairs_of = [pairs, [pairs[m ^ 2] for m in range(n_member)]]
    owner_of = [[0] * n_chip for _ in range(2)]
    slot_of = [[0] * n_chip for _ in range(2)]
    for par in range(2):
        for m, pair in enumerate(pairs_of[par]):
            for a, off in enumerate(pair):
                owner_of[par][off] = m
                slot_of[par][off] = a
    own = []
    for a in range(chips_per_dev):
        perm = []
        for m in range(n_member):
            for s in range(n_space):
                p = s // 2
                src = 2 * ((p + pairs_of[p % 2][m][a]) % n_chip) + s % 2
                perm.append((m * n_space + src, m * n_space + s))
        assert len({src for src, _ in perm}) == len(perm)
        if a == 0:
            half_reg = reg_count // 2
            first = lax.ppermute(weights[:half_reg], ("member", "space"), perm)
            rest = lax.ppermute(weights[half_reg:], ("member", "space"), perm)
            own.append(None)
        else:
            own.append(lax.ppermute(weights, ("member", "space"), perm))
    sib_perm = [(m * n_space + s, m * n_space + (s ^ 1)) for m in range(n_member) for s in range(n_space)]

    group = region_ids // reg_count
    offset = (group // 2 - chip) % n_chip
    par = chip % 2
    half_ring = ring // 2

    def owner_slot(o, p, xp):
        r = o % ring
        base = xp.where(r == half_ring, 0, xp.where(r < half_ring, r, ring - r))
        return xp.bitwise_xor(base + half_ring * (o // ring), 2 * p), (r >= half_ring).astype(xp.int32)

    for p_ in range(2):
        o_ = np.arange(n_chip)
        m_, a_ = owner_slot(o_, p_, np)
        assert list(m_) == owner_of[p_] and list(a_) == slot_of[p_]
    dest, slot_a = owner_slot(offset, par, jnp)
    slot = (group % 2 != core).astype(jnp.int32) * chips_per_dev + slot_a
    group_hot = (group[:, None] == jnp.arange(n_space, dtype=jnp.int32)[None, :]).astype(jnp.int32)
    before = jnp.cumsum(group_hot, axis=0) - group_hot
    rank_in = jnp.sum(before * group_hot, axis=1)
    position = dest * own_cols + slot * send_cols + rank_in
    label = slot * reg_count + region_ids % reg_count
    pos_iota = jnp.arange(columns, dtype=jnp.int32)
    perm_hot = position[:, None] == pos_iota[None, :]
    perm_mat = perm_hot.astype(jnp.bfloat16).reshape(columns, n_member, own_cols)
    label_sorted = jnp.sum(jnp.where(perm_hot, label[:, None], 0), axis=0).reshape(n_member, own_cols)
    my_labels = lax.dynamic_index_in_dim(label_sorted, me_member, 0, keepdims=False)

    region_hot = (jnp.arange(all_regions, dtype=jnp.int32)[:, None] == region_ids[None, :]).astype(
        jnp.float32
    )
    factor = jnp.dot(inflation, region_hot, precision=lax.Precision.HIGHEST)
    fac_perm = jnp.einsum(
        "jc,cdi->dji", factor, perm_mat.astype(jnp.float32), precision=lax.Precision.HIGHEST
    )
    flat = tracers * own_cols
    main = jnp.einsum("jtc,cdi->djti", ensemble, perm_mat, preferred_element_type=jnp.bfloat16)
    main = main.reshape(n_member, local_members, flat)
    hi, mid, lo = _split3(fac_perm)
    spare = 128 - (3 * own_cols) % 128
    pad = jnp.zeros((n_member, local_members, spare), jnp.bfloat16)
    payload = jnp.concatenate([main, hi, mid, lo, pad], axis=2)

    payload, first = lax.optimization_barrier((payload, first))
    own = jnp.stack([jnp.concatenate([first, rest], axis=0)] + own[1:])
    sib = lax.ppermute(own, ("member", "space"), sib_perm)
    w_all = jnp.concatenate([own, sib], axis=0).reshape(n_slot, members, members)
    received = lax.all_to_all(payload, "member", split_axis=0, concat_axis=0, tiled=True)
    received = received.reshape(members, payload.shape[2])
    ens32 = received[:, :flat].astype(jnp.float32)
    got = received[:, flat:].astype(jnp.float32)
    fac = (got[:, 0:own_cols] + got[:, own_cols:2 * own_cols]) + got[:, 2 * own_cols:3 * own_cols]
    lane_col = jnp.arange(flat, dtype=jnp.int32) % own_cols
    spread = (jnp.arange(own_cols, dtype=jnp.int32)[:, None] == lane_col[None, :]).astype(jnp.float32)
    fac_wide = jnp.dot(fac, spread, precision=lax.Precision.HIGHEST)
    mean = jnp.sum(ens32, axis=0) / members
    anomaly = ((ens32 - mean[None]) * fac_wide).astype(jnp.bfloat16)
    mask = my_labels[None, :] == jnp.arange(n_slot, dtype=jnp.int32)[:, None]
    mask = jnp.tile(mask, (1, tracers))
    masked = jnp.where(mask[:, None, :], anomaly[None], jnp.zeros((), jnp.bfloat16))
    inc = jnp.einsum("rjk,rjx->kx", w_all, masked, preferred_element_type=jnp.float32)
    inc = lax.reduce_precision(inc, exponent_bits=8, mantissa_bits=7)
    result = (mean[None] + inc).astype(jnp.bfloat16)
    result = result.reshape(n_member, local_members, flat)
    returned = lax.all_to_all(result, "member", split_axis=0, concat_axis=0, tiled=True)
    returned = returned.reshape(n_member, local_members, tracers, own_cols)
    rows = returned.reshape(n_member, local_members * tracers, own_cols)
    analysis = jnp.einsum("dni,cdi->nc", rows, perm_mat, preferred_element_type=jnp.bfloat16)
    analysis = analysis.reshape(local_members, tracers, columns)

    local_index = obs_cols - me_space * columns
    obs_pos = jnp.take(position, local_index)
    obs_mat = (pos_iota[:, None] == obs_pos[None, :]).astype(jnp.bfloat16)
    obs_mat = obs_mat.reshape(n_member, own_cols, obs_cols.shape[0])
    picked = jnp.einsum("dni,dio->no", rows, obs_mat, preferred_element_type=jnp.float32)
    picked = picked.reshape(local_members, tracers, obs_cols.shape[0])
    obs_analysis = jnp.einsum("t,kto->ko", extinction, picked, precision=lax.Precision.HIGHEST)
    return (analysis, obs_analysis)


def solution(mesh):
    in_specs = (
        P("member", None, "space"),
        P("member", None),
        P("space", None, None),
        P("space"),
        P(),
        P("space"),
    )
    out_specs = (P("member", None, "space"), P("member", "space"))
    return jax.shard_map(local, mesh=mesh, in_specs=in_specs, out_specs=out_specs, check_vma=False)
```

```python
import jax
import numpy as np
import jax.numpy as jnp
from jax import lax
from jax.sharding import PartitionSpec as P


def _split3(x):
    hi = lax.reduce_precision(x, exponent_bits=8, mantissa_bits=7)
    r1 = x - hi
    mid = lax.reduce_precision(r1, exponent_bits=8, mantissa_bits=7)
    lo = r1 - mid
    return hi.astype(jnp.bfloat16), mid.astype(jnp.bfloat16), lo.astype(jnp.bfloat16)


def local(ensemble, inflation, weights, region_ids, extinction, obs_cols):
    n_space = lax.axis_size("space")
    n_member = lax.axis_size("member")
    local_members, tracers, columns = ensemble.shape
    members = local_members * n_member
    reg_count = weights.shape[0]
    all_regions = inflation.shape[1]
    groups_per_dev = n_space // n_member
    send_cols = columns // n_space
    own_cols = columns // n_member
    n_chip = n_space // 2
    chips_per_dev = groups_per_dev // 2
    n_slot = groups_per_dev * reg_count
    me_space = lax.axis_index("space")
    me_member = lax.axis_index("member")
    chip = me_space // 2
    core = me_space % 2

    ring = n_chip // 2
    pairs = [(0, ring // 2)] + [(b, ring - b) for b in range(1, ring // 2)]
    pairs = pairs + [(a + ring, b + ring) for a, b in pairs]
    pairs_of = [pairs, [pairs[m ^ 2] for m in range(n_member)]]
    owner_of = [[0] * n_chip for _ in range(2)]
    slot_of = [[0] * n_chip for _ in range(2)]
    for par in range(2):
        for m, pair in enumerate(pairs_of[par]):
            for a, off in enumerate(pair):
                owner_of[par][off] = m
                slot_of[par][off] = a
    own = []
    for a in range(chips_per_dev):
        perm = []
        for m in range(n_member):
            for s in range(n_space):
                p = s // 2
                src = 2 * ((p + pairs_of[p % 2][m][a]) % n_chip) + s % 2
                perm.append((m * n_space + src, m * n_space + s))
        assert len({src for src, _ in perm}) == len(perm)
        if a == 0:
            half_reg = 1
            first = lax.ppermute(weights[:half_reg], ("member", "space"), perm)
            rest = lax.ppermute(weights[half_reg:], ("member", "space"), perm)
            own.append(None)
        else:
            own.append(lax.ppermute(weights, ("member", "space"), perm))
    sib_perm = [(m * n_space + s, m * n_space + (s ^ 1)) for m in range(n_member) for s in range(n_space)]

    group = region_ids // reg_count
    offset = (group // 2 - chip) % n_chip
    par = chip % 2
    half_ring = ring // 2

    def owner_slot(o, p, xp):
        r = o % ring
        base = xp.where(r == half_ring, 0, xp.where(r < half_ring, r, ring - r))
        return xp.bitwise_xor(base + half_ring * (o // ring), 2 * p), (r >= half_ring).astype(xp.int32)

    for p_ in range(2):
        o_ = np.arange(n_chip)
        m_, a_ = owner_slot(o_, p_, np)
        assert list(m_) == owner_of[p_] and list(a_) == slot_of[p_]
    dest, slot_a = owner_slot(offset, par, jnp)
    slot = (group % 2 != core).astype(jnp.int32) * chips_per_dev + slot_a
    group_hot = (group[:, None] == jnp.arange(n_space, dtype=jnp.int32)[None, :]).astype(jnp.int32)
    before = jnp.cumsum(group_hot, axis=0) - group_hot
    rank_in = jnp.sum(before * group_hot, axis=1)
    position = dest * own_cols + slot * send_cols + rank_in
    label = slot * reg_count + region_ids % reg_count
    pos_iota = jnp.arange(columns, dtype=jnp.int32)
    perm_hot = position[:, None] == pos_iota[None, :]
    perm_mat = perm_hot.astype(jnp.bfloat16).reshape(columns, n_member, own_cols)
    label_sorted = jnp.sum(jnp.where(perm_hot, label[:, None], 0), axis=0).reshape(n_member, own_cols)
    my_labels = lax.dynamic_index_in_dim(label_sorted, me_member, 0, keepdims=False)

    region_hot = (jnp.arange(all_regions, dtype=jnp.int32)[:, None] == region_ids[None, :]).astype(
        jnp.float32
    )
    factor = jnp.dot(inflation, region_hot, precision=lax.Precision.HIGHEST)
    fac_perm = jnp.einsum(
        "jc,cdi->dji", factor, perm_mat.astype(jnp.float32), precision=lax.Precision.HIGHEST
    )
    flat = tracers * own_cols
    main = jnp.einsum("jtc,cdi->djti", ensemble, perm_mat, preferred_element_type=jnp.bfloat16)
    main = main.reshape(n_member, local_members, flat)
    hi, mid, lo = _split3(fac_perm)
    spare = 128 - (3 * own_cols) % 128
    pad = jnp.zeros((n_member, local_members, spare), jnp.bfloat16)
    payload = jnp.concatenate([main, hi, mid, lo, pad], axis=2)

    payload, first = lax.optimization_barrier((payload, first))
    own = jnp.stack([jnp.concatenate([first, rest], axis=0)] + own[1:])
    sib = lax.ppermute(own, ("member", "space"), sib_perm)
    w_all = jnp.concatenate([own, sib], axis=0).reshape(n_slot, members, members)
    received = lax.all_to_all(payload, "member", split_axis=0, concat_axis=0, tiled=True)
    received = received.reshape(members, payload.shape[2])
    ens32 = received[:, :flat].astype(jnp.float32)
    got = received[:, flat:].astype(jnp.float32)
    fac = (got[:, 0:own_cols] + got[:, own_cols:2 * own_cols]) + got[:, 2 * own_cols:3 * own_cols]
    lane_col = jnp.arange(flat, dtype=jnp.int32) % own_cols
    spread = (jnp.arange(own_cols, dtype=jnp.int32)[:, None] == lane_col[None, :]).astype(jnp.float32)
    fac_wide = jnp.dot(fac, spread, precision=lax.Precision.HIGHEST)
    mean = jnp.sum(ens32, axis=0) / members
    anomaly = ((ens32 - mean[None]) * fac_wide).astype(jnp.bfloat16)
    mask = my_labels[None, :] == jnp.arange(n_slot, dtype=jnp.int32)[:, None]
    mask = jnp.tile(mask, (1, tracers))
    masked = jnp.where(mask[:, None, :], anomaly[None], jnp.zeros((), jnp.bfloat16))
    inc = jnp.einsum("rjk,rjx->kx", w_all, masked, preferred_element_type=jnp.float32)
    inc = lax.reduce_precision(inc, exponent_bits=8, mantissa_bits=7)
    result = (mean[None] + inc).astype(jnp.bfloat16)
    result = result.reshape(n_member, local_members, flat)
    returned = lax.all_to_all(result, "member", split_axis=0, concat_axis=0, tiled=True)
    returned = returned.reshape(n_member, local_members, tracers, own_cols)
    rows = returned.reshape(n_member, local_members * tracers, own_cols)
    analysis = jnp.einsum("dni,cdi->nc", rows, perm_mat, preferred_element_type=jnp.bfloat16)
    analysis = analysis.reshape(local_members, tracers, columns)

    local_index = obs_cols - me_space * columns
    obs_pos = jnp.take(position, local_index)
    obs_mat = (pos_iota[:, None] == obs_pos[None, :]).astype(jnp.bfloat16)
    obs_mat = obs_mat.reshape(n_member, own_cols, obs_cols.shape[0])
    picked = jnp.einsum("dni,dio->no", rows, obs_mat, preferred_element_type=jnp.float32)
    picked = picked.reshape(local_members, tracers, obs_cols.shape[0])
    obs_analysis = jnp.einsum("t,kto->ko", extinction, picked, precision=lax.Precision.HIGHEST)
    return (analysis, obs_analysis)


def solution(mesh):
    in_specs = (
        P("member", None, "space"),
        P("member", None),
        P("space", None, None),
        P("space"),
        P(),
        P("space"),
    )
    out_specs = (P("member", None, "space"), P("member", "space"))
    return jax.shard_map(local, mesh=mesh, in_specs=in_specs, out_specs=out_specs, check_vma=False)
```
